512 devices in a mesh: dp: 16 (over x, y), seq: 32 (over z, core).
Axes of the slice: x: 4, y: 4, z: 16, core: 2. Of those that a mesh axis runs over, the one named last changes fastest.
Arguments:
- query_rows: bfloat16 [32, 2048, 2048], P('seq', 'dp'), may hold values from -8 to 8
- key_rows: bfloat16 [32, 2048, 2048], P('seq', 'dp'), may hold values from -8 to 8
- value_rows: bfloat16 [32, 2048, 2048], P('seq', 'dp'), may hold values from -6 to 6
- out_grad: bfloat16 [32, 2048, 3072], P('seq', 'dp'), may hold values from -96 to 96
- out_weight: bfloat16 [2, 2048, 3072], P(None, ('dp', 'seq')), may hold values from -0.125 to 0.125
- text_length: int32 [32], P('seq'), may hold values from 65 to 512
Outputs:
- query_grad: bfloat16 [32, 2048, 2048], P('seq', 'dp')
- key_grad: bfloat16 [32, 2048, 2048], P('seq', 'dp')
- value_grad: bfloat16 [32, 2048, 2048], P('seq', 'dp')
The draws below stay inside these ranges and needn't reach their ends.
All inputs are finite; a program needn't handle non-finite values.
Results may differ from the reference program's by a relative error of at most 0.0076.
Values may be sent and summed in bfloat16 or wider, within the bound.
No kernel may reach another device: no remote copies, remote signals or barrier semaphores. Data moves between devices by JAX's collectives and lax.ppermute only.
A program may use at most 128 MiB of HBM per device.

```python
import math
import jax
import jax.numpy as jnp
from jax import lax

D = 3072
HEADS = 16
HEAD_DIM = 128
TXT = 512
HW = 2048
L = 2048
SAMPLES = 32


def attention_inputs(key):
    shape = (SAMPLES, L, HW)
    query_draw = jax.random.truncated_normal(jax.random.fold_in(key, 201), -6.0, 6.0, shape, jnp.float32)
    key_draw = jax.random.truncated_normal(jax.random.fold_in(key, 202), -6.0, 6.0, shape, jnp.float32)
    return (query_draw, key_draw)


def draw_query_rows(key, part):
    return attention_inputs(key)[0].astype(jnp.bfloat16)


def draw_key_rows(key, part):
    return attention_inputs(key)[1].astype(jnp.bfloat16)


def draw_text_length(key, part):
    lowest = TXT // 8 + 1
    values = jax.random.randint(jax.random.fold_in(key, 301), (SAMPLES,), lowest, TXT + 1)
    longest = jax.random.randint(jax.random.fold_in(key, 302), (), 0, SAMPLES)
    shortest = (longest + 1 + jax.random.randint(jax.random.fold_in(key, 303), (), 0, SAMPLES - 1)) % SAMPLES
    sample_index = jnp.arange(SAMPLES)
    values = jnp.where(sample_index == longest, TXT, values)
    values = jnp.where(sample_index == shortest, lowest, values)
    return values.astype(jnp.int32)


def block_scale(stream_key, extent, shards, low, largest):
    def one(dim, blocks):
        heights = jax.random.uniform(jax.random.fold_in(jax.random.fold_in(stream_key, 6), dim), (blocks,), jnp.float32, low / len(shards), largest / len(shards))
        return jnp.repeat(jnp.exp(heights), extent[dim] // blocks).reshape((-1,) + (1,) * (len(extent) - dim - 1))

    level = one(*shards[0])
    for cut in shards[1:]:
        level = level * one(*cut)
    return level


def scatter_about(own_key, shape, spread, most, cuts=(), held_as=jnp.bfloat16):
    drawn = jax.random.normal(own_key, shape, jnp.float32) * spread
    if len(cuts) > 0:
        drawn = block_scale(own_key, shape, cuts, -0.22, 0.18) * drawn
    return jnp.clip(drawn, min=-most, max=most).astype(held_as)


def setup_inputs(seed: int = 0) -> dict:
    key_of = jax.random.split(jax.random.key(seed), 7)
    return {
        "query_rows": draw_query_rows(jax.random.fold_in(key_of[6], 71), 0),
        "key_rows": draw_key_rows(jax.random.fold_in(key_of[6], 71), 0),
        "value_rows": scatter_about(key_of[2], (SAMPLES, L, HW), 1.0, 6.0, ((0, 32), (1, 16))),
        "out_grad": scatter_about(key_of[3], (SAMPLES, L, D), 16.0, 96.0, ((0, 32), (1, 16))),
        "out_weight": scatter_about(key_of[4], (2, HW, D), HW ** -0.5, 0.125, ((1, 512),)),
        "text_length": draw_text_length(jax.random.fold_in(key_of[6], 71), 0),
    }


def head_grads(query_head, key_head, value_head, grad_head, key_valid):
    factor = 1.0 / math.sqrt(HEAD_DIM)
    scores = jnp.dot(query_head, key_head.T, preferred_element_type=jnp.float32) * factor
    scores = jnp.where(key_valid[None, :], scores, -jnp.inf)
    shifted = jnp.exp(scores - lax.optimization_barrier(jnp.max(scores, axis=1, keepdims=True)))
    attention = shifted / lax.optimization_barrier(jnp.sum(shifted, axis=1, keepdims=True))
    value_grad = jnp.dot(attention.astype(jnp.bfloat16).T, grad_head, preferred_element_type=jnp.float32).astype(jnp.bfloat16)
    weight_grad = jnp.dot(grad_head, value_head.T, preferred_element_type=jnp.float32)
    row_dot = lax.optimization_barrier(jnp.sum(attention * weight_grad, axis=1, keepdims=True))
    score_grad = (attention * (weight_grad - row_dot) * factor).astype(jnp.bfloat16)
    query_grad = jnp.dot(score_grad, key_head, preferred_element_type=jnp.float32).astype(jnp.bfloat16)
    key_grad = jnp.dot(score_grad.T, query_head, preferred_element_type=jnp.float32).astype(jnp.bfloat16)
    return (query_grad, key_grad, value_grad)

def reference(query_rows, key_rows, value_rows, out_grad, out_weight, text_length):
    positions = jnp.arange(L).astype(jnp.int32)

    def split_heads(array):
        return array.reshape(L, HEADS, HEAD_DIM).transpose(1, 0, 2)

    def join_heads(array):
        return array.transpose(1, 0, 2).reshape(L, HEADS * HEAD_DIM)

    def one_sample(operands):
        query_one, key_one, value_one, cotangent, length = operands
        text_part = jnp.dot(cotangent[:TXT], out_weight[0].T, preferred_element_type=jnp.float32)
        image_part = jnp.dot(cotangent[TXT:], out_weight[1].T, preferred_element_type=jnp.float32)
        grad_heads = jnp.concatenate([text_part, image_part], axis=0).astype(jnp.bfloat16)
        key_valid = (positions >= TXT) | (positions < length)

        def one_head(pieces):
            return head_grads(pieces[0], pieces[1], pieces[2], pieces[3], key_valid)
        grads = lax.map(one_head, (split_heads(query_one), split_heads(key_one), split_heads(value_one), split_heads(grad_heads)))
        return (join_heads(grads[0]), join_heads(grads[1]), join_heads(grads[2]))
    query_grad, key_grad, value_grad = lax.map(one_sample, (query_rows, key_rows, value_rows, out_grad, text_length))
    return (query_grad, key_grad, value_grad)
```

```python
import functools
import math

import jax
import jax.numpy as jnp
from jax import lax
from jax.experimental import pallas as pl
from jax.experimental.pallas import tpu as pltpu
from jax.sharding import PartitionSpec as P

HEADS = 16
HEAD_DIM = 128
TXT = 512
BLOCK_ROWS = 256


def attention_kernel(length_ref, q_ref, k_ref, v_ref, g_ref, dq_ref, dk_ref, dv_ref, dkt_acc, dvt_acc):
    step = pl.program_id(0)
    factor = 1.0 / math.sqrt(q_ref.shape[1])
    nt = (((1,), (1,)), ((), ()))

    @pl.when(step == 0)
    def _():
        dkt_acc[...] = jnp.zeros_like(dkt_acc)
        dvt_acc[...] = jnp.zeros_like(dvt_acc)

    query_block = q_ref[...]
    grad_block = g_ref[...]
    keys = k_ref[...]
    values = v_ref[...]
    scores = lax.dot_general(query_block, keys, nt, preferred_element_type=jnp.float32) * factor
    column = lax.broadcasted_iota(jnp.int32, scores.shape, 1)
    valid = (column >= TXT) | (column < length_ref[0])
    scores = jnp.where(valid, scores, -jnp.inf)
    shifted = jnp.exp(scores - jnp.max(scores, axis=1, keepdims=True))
    attention = shifted / jnp.sum(shifted, axis=1, keepdims=True)
    attention_low = attention.astype(jnp.bfloat16)
    grad_t = grad_block.astype(jnp.float32).T.astype(jnp.bfloat16)
    dvt_acc[...] += jnp.dot(grad_t, attention_low, preferred_element_type=jnp.float32)
    weight_grad = lax.dot_general(grad_block, values, nt, preferred_element_type=jnp.float32)
    row_dot = jnp.sum(attention * weight_grad, axis=1, keepdims=True)
    score_grad = (attention * (weight_grad - row_dot) * factor).astype(jnp.bfloat16)
    dq_ref[...] = jnp.dot(score_grad, keys, preferred_element_type=jnp.float32).astype(dq_ref.dtype)
    query_t = query_block.astype(jnp.float32).T.astype(jnp.bfloat16)
    dkt_acc[...] += jnp.dot(query_t, score_grad, preferred_element_type=jnp.float32)

    @pl.when(step == pl.num_programs(0) - 1)
    def _():
        dk_ref[...] = dkt_acc[...].T.astype(dk_ref.dtype)
        dv_ref[...] = dvt_acc[...].T.astype(dv_ref.dtype)


def attention_grads(query, key, value, grad, length):
    rows, width = query.shape
    block = min(BLOCK_ROWS, rows)
    row_spec = pl.BlockSpec((block, width), lambda i: (i, 0))
    full_spec = pl.BlockSpec((rows, width), lambda i: (0, 0))
    out = jax.ShapeDtypeStruct((rows, width), jnp.bfloat16)
    flops = 10 * rows * rows * width
    return pl.pallas_call(
        attention_kernel,
        grid=(rows // block,),
        in_specs=[
            pl.BlockSpec(memory_space=pltpu.SMEM),
            row_spec,
            full_spec,
            full_spec,
            row_spec,
        ],
        out_specs=[row_spec, full_spec, full_spec],
        out_shape=[out, out, out],
        scratch_shapes=[
            pltpu.VMEM((width, rows), jnp.float32),
            pltpu.VMEM((width, rows), jnp.float32),
        ],
        compiler_params=pltpu.CompilerParams(
            dimension_semantics=("arbitrary",), vmem_limit_bytes=48 * 1024 * 1024
        ),
        cost_estimate=pl.CostEstimate(
            flops=flops, transcendentals=rows * rows, bytes_accessed=7 * rows * width * 2
        ),
    )(length, query, key, value, grad)


def per_device(query_rows, key_rows, value_rows, out_grad, out_weight, text_length):
    devices = lax.axis_size("dp")
    tok_rows = query_rows.shape[1]

    def by_heads(array):
        return array[0].reshape(tok_rows, HEADS, HEAD_DIM)

    both_streams = lax.all_gather(out_weight, "dp", axis=1, tiled=False)
    stream = (lax.axis_index("dp") * tok_rows >= TXT).astype(jnp.int32)
    stream_rows = lax.dynamic_index_in_dim(both_streams, stream, 0, keepdims=False)
    weight = lax.all_gather(stream_rows, "seq", axis=1, tiled=True)

    qkv = jnp.stack([by_heads(query_rows), by_heads(key_rows), by_heads(value_rows)])
    qkv_heads = lax.all_to_all(qkv, "dp", split_axis=2, concat_axis=1, tiled=True)

    projected = jnp.einsum(
        "te,kre->tkr", out_grad[0], weight, preferred_element_type=jnp.float32
    )
    grad_heads = lax.all_to_all(
        projected.astype(jnp.bfloat16), "dp", split_axis=1, concat_axis=0, tiled=True
    )
    total_rows = tok_rows * devices
    query_grad, key_grad, value_grad = attention_grads(
        qkv_heads[0].reshape(total_rows, HEAD_DIM),
        qkv_heads[1].reshape(total_rows, HEAD_DIM),
        qkv_heads[2].reshape(total_rows, HEAD_DIM),
        grad_heads.reshape(total_rows, HEAD_DIM),
        text_length,
    )
    grads = jnp.stack([query_grad, key_grad, value_grad]).reshape(3, total_rows, 1, HEAD_DIM)
    returned = lax.all_to_all(grads, "dp", split_axis=1, concat_axis=2, tiled=True)
    returned = returned.reshape(3, 1, tok_rows, HEADS * HEAD_DIM)
    return (returned[0], returned[1], returned[2])


def solution(mesh):
    in_specs = (
        P("seq", "dp", None),
        P("seq", "dp", None),
        P("seq", "dp", None),
        P("seq", "dp", None),
        P(None, ("dp", "seq"), None),
        P("seq"),
    )
    out_specs = (P("seq", "dp", None), P("seq", "dp", None), P("seq", "dp", None))
    return jax.shard_map(
        per_device, mesh=mesh, in_specs=in_specs, out_specs=out_specs, check_vma=False
    )
```

```python
import functools
import math

import jax
import jax.numpy as jnp
from jax import lax
from jax.experimental import pallas as pl
from jax.experimental.pallas import tpu as pltpu
from jax.sharding import PartitionSpec as P

HEADS = 16
HEAD_DIM = 128
TXT = 512
BLOCK_ROWS = 256


def attention_kernel(length_ref, q_ref, k_ref, v_ref, g_ref, dq_ref, dk_ref, dv_ref, dkt_acc, dvt_acc):
    step = pl.program_id(0)
    factor = 1.0 / math.sqrt(q_ref.shape[1])
    nt = (((1,), (1,)), ((), ()))

    @pl.when(step == 0)
    def _():
        dkt_acc[...] = jnp.zeros_like(dkt_acc)
        dvt_acc[...] = jnp.zeros_like(dvt_acc)

    query_block = q_ref[...]
    grad_block = g_ref[...]
    keys = k_ref[...]
    values = v_ref[...]
    scores = lax.dot_general(query_block, keys, nt, preferred_element_type=jnp.float32) * factor
    column = lax.broadcasted_iota(jnp.int32, scores.shape, 1)
    valid = (column >= TXT) | (column < length_ref[0])
    scores = jnp.where(valid, scores, -jnp.inf)
    shifted = jnp.exp(scores - jnp.max(scores, axis=1, keepdims=True))
    attention = shifted / jnp.sum(shifted, axis=1, keepdims=True)
    attention_low = attention.astype(jnp.bfloat16)
    grad_t = grad_block.astype(jnp.float32).T.astype(jnp.bfloat16)
    dvt_acc[...] += jnp.dot(grad_t, attention_low, preferred_element_type=jnp.float32)
    weight_grad = lax.dot_general(grad_block, values, nt, preferred_element_type=jnp.float32)
    row_dot = jnp.sum(attention * weight_grad, axis=1, keepdims=True)
    score_grad = (attention * (weight_grad - row_dot) * factor).astype(jnp.bfloat16)
    dq_ref[...] = jnp.dot(score_grad, keys, preferred_element_type=jnp.float32).astype(dq_ref.dtype)
    query_t = query_block.astype(jnp.float32).T.astype(jnp.bfloat16)
    dkt_acc[...] += jnp.dot(query_t, score_grad, preferred_element_type=jnp.float32)

    @pl.when(step == pl.num_programs(0) - 1)
    def _():
        dk_ref[...] = dkt_acc[...].T.astype(dk_ref.dtype)
        dv_ref[...] = dvt_acc[...].T.astype(dv_ref.dtype)


def attention_grads(query, key, value, grad, length):
    rows, width = query.shape
    block = min(BLOCK_ROWS, rows)
    row_spec = pl.BlockSpec((block, width), lambda i: (i, 0))
    full_spec = pl.BlockSpec((rows, width), lambda i: (0, 0))
    out = jax.ShapeDtypeStruct((rows, width), jnp.bfloat16)
    flops = 10 * rows * rows * width
    return pl.pallas_call(
        attention_kernel,
        grid=(rows // block,),
        in_specs=[
            pl.BlockSpec(memory_space=pltpu.SMEM),
            row_spec,
            full_spec,
            full_spec,
            row_spec,
        ],
        out_specs=[row_spec, full_spec, full_spec],
        out_shape=[out, out, out],
        scratch_shapes=[
            pltpu.VMEM((width, rows), jnp.float32),
            pltpu.VMEM((width, rows), jnp.float32),
        ],
        compiler_params=pltpu.CompilerParams(
            dimension_semantics=("arbitrary",), vmem_limit_bytes=48 * 1024 * 1024
        ),
        cost_estimate=pl.CostEstimate(
            flops=flops, transcendentals=rows * rows, bytes_accessed=7 * rows * width * 2
        ),
    )(length, query, key, value, grad)


def projection_kernel(grad_ref, weight_ref, out_ref):
    nt = (((1,), (1,)), ((), ()))
    out_ref[0] = lax.dot_general(
        grad_ref[...], weight_ref[0], nt, preferred_element_type=jnp.float32
    ).astype(out_ref.dtype)


def project(out_grad, weight):
    rows, depth = out_grad.shape
    heads, width, _ = weight.shape
    return pl.pallas_call(
        projection_kernel,
        grid=(heads,),
        in_specs=[
            pl.BlockSpec((rows, depth), lambda h: (0, 0)),
            pl.BlockSpec((1, width, depth), lambda h: (h, 0, 0)),
        ],
        out_specs=pl.BlockSpec((1, rows, width), lambda h: (h, 0, 0)),
        out_shape=jax.ShapeDtypeStruct((heads, rows, width), jnp.bfloat16),
        compiler_params=pltpu.CompilerParams(dimension_semantics=("arbitrary",)),
        cost_estimate=pl.CostEstimate(
            flops=2 * rows * depth * heads * width,
            transcendentals=0,
            bytes_accessed=(rows * depth + heads * width * depth + heads * rows * width) * 2,
        ),
    )(out_grad, weight)


def per_device(query_rows, key_rows, value_rows, out_grad, out_weight, text_length):
    devices = lax.axis_size("dp")
    tok_rows = query_rows.shape[1]

    def by_heads(array):
        return array[0].reshape(tok_rows, HEADS, HEAD_DIM)

    slot_text = (jnp.arange(devices) * tok_rows < TXT)[:, None, None]
    outgoing = jnp.where(slot_text, out_weight[0][None], out_weight[1][None])
    stream_rows = lax.all_to_all(outgoing, "dp", split_axis=0, concat_axis=0, tiled=True)
    weight = lax.all_gather(stream_rows, "seq", axis=1, tiled=True)

    qkv = jnp.stack([by_heads(query_rows), by_heads(key_rows), by_heads(value_rows)])
    qkv_heads = lax.all_to_all(qkv, "dp", split_axis=2, concat_axis=1, tiled=True)

    projected = project(out_grad[0], weight)
    grad_heads = lax.all_to_all(projected, "dp", split_axis=0, concat_axis=0, tiled=True)
    total_rows = tok_rows * devices
    query_grad, key_grad, value_grad = attention_grads(
        qkv_heads[0].reshape(total_rows, HEAD_DIM),
        qkv_heads[1].reshape(total_rows, HEAD_DIM),
        qkv_heads[2].reshape(total_rows, HEAD_DIM),
        grad_heads.reshape(total_rows, HEAD_DIM),
        text_length,
    )
    returned = [
        lax.all_to_all(
            grad.reshape(total_rows, 1, HEAD_DIM), "dp", split_axis=0, concat_axis=1, tiled=True
        ).reshape(1, tok_rows, HEADS * HEAD_DIM)
        for grad in (query_grad, key_grad, value_grad)
    ]
    return tuple(returned)


def solution(mesh):
    in_specs = (
        P("seq", "dp", None),
        P("seq", "dp", None),
        P("seq", "dp", None),
        P("seq", "dp", None),
        P(None, ("dp", "seq"), None),
        P("seq"),
    )
    out_specs = (P("seq", "dp", None), P("seq", "dp", None), P("seq", "dp", None))
    return jax.shard_map(
        per_device, mesh=mesh, in_specs=in_specs, out_specs=out_specs, check_vma=False
    )
```

```python
import functools
import math

import jax
import jax.numpy as jnp
from jax import lax
from jax.experimental import pallas as pl
from jax.experimental.pallas import tpu as pltpu
from jax.sharding import PartitionSpec as P

HEADS = 16
HEAD_DIM = 128
TXT = 512
BLOCK_ROWS = 256


def attention_kernel(length_ref, q_ref, k_ref, v_ref, g_ref, dq_ref, dk_ref, dv_ref, dkt_acc, dvt_acc):
    step = pl.program_id(0)
    factor = 1.0 / math.sqrt(q_ref.shape[1])
    nt = (((1,), (1,)), ((), ()))

    @pl.when(step == 0)
    def _():
        dkt_acc[...] = jnp.zeros_like(dkt_acc)
        dvt_acc[...] = jnp.zeros_like(dvt_acc)

    query_block = q_ref[...]
    grad_block = g_ref[...]
    keys = k_ref[...]
    values = v_ref[...]
    scores = lax.dot_general(query_block, keys, nt, preferred_element_type=jnp.float32) * factor
    column = lax.broadcasted_iota(jnp.int32, scores.shape, 1)
    valid = (column >= TXT) | (column < length_ref[0])
    scores = jnp.where(valid, scores, -jnp.inf)
    shifted = jnp.exp(scores - jnp.max(scores, axis=1, keepdims=True))
    attention = shifted / jnp.sum(shifted, axis=1, keepdims=True)
    attention_low = attention.astype(jnp.bfloat16)
    grad_t = grad_block.astype(jnp.float32).T.astype(jnp.bfloat16)
    dvt_acc[...] += jnp.dot(grad_t, attention_low, preferred_element_type=jnp.float32)
    weight_grad = lax.dot_general(grad_block, values, nt, preferred_element_type=jnp.float32)
    row_dot = jnp.sum(attention * weight_grad, axis=1, keepdims=True)
    score_grad = (attention * (weight_grad - row_dot) * factor).astype(jnp.bfloat16)
    dq_ref[...] = jnp.dot(score_grad, keys, preferred_element_type=jnp.float32).astype(dq_ref.dtype)
    query_t = query_block.astype(jnp.float32).T.astype(jnp.bfloat16)
    dkt_acc[...] += jnp.dot(query_t, score_grad, preferred_element_type=jnp.float32)

    @pl.when(step == pl.num_programs(0) - 1)
    def _():
        dk_ref[...] = dkt_acc[...].T.astype(dk_ref.dtype)
        dv_ref[...] = dvt_acc[...].T.astype(dv_ref.dtype)


def attention_grads(query, key, value, grad, length):
    rows, width = query.shape
    block = min(BLOCK_ROWS, rows)
    row_spec = pl.BlockSpec((block, width), lambda i: (i, 0))
    full_spec = pl.BlockSpec((rows, width), lambda i: (0, 0))
    out = jax.ShapeDtypeStruct((rows, width), jnp.bfloat16)
    flops = 10 * rows * rows * width
    return pl.pallas_call(
        attention_kernel,
        grid=(rows // block,),
        in_specs=[
            pl.BlockSpec(memory_space=pltpu.SMEM),
            row_spec,
            full_spec,
            full_spec,
            row_spec,
        ],
        out_specs=[row_spec, full_spec, full_spec],
        out_shape=[out, out, out],
        scratch_shapes=[
            pltpu.VMEM((width, rows), jnp.float32),
            pltpu.VMEM((width, rows), jnp.float32),
        ],
        compiler_params=pltpu.CompilerParams(
            dimension_semantics=("arbitrary",), vmem_limit_bytes=48 * 1024 * 1024
        ),
        cost_estimate=pl.CostEstimate(
            flops=flops, transcendentals=rows * rows, bytes_accessed=7 * rows * width * 2
        ),
    )(length, query, key, value, grad)


def per_device(query_rows, key_rows, value_rows, out_grad, out_weight, text_length):
    devices = lax.axis_size("dp")
    tok_rows = query_rows.shape[1]

    def by_heads(array):
        return array[0].reshape(tok_rows, HEADS, HEAD_DIM)

    slot_text = (jnp.arange(devices) * tok_rows < TXT)[:, None, None]
    outgoing = jnp.where(slot_text, out_weight[0][None], out_weight[1][None])
    stream_rows = lax.all_to_all(outgoing, "dp", split_axis=0, concat_axis=0, tiled=True)
    weight = lax.all_gather(stream_rows, "seq", axis=1, tiled=True)

    qkv = jnp.stack([by_heads(query_rows), by_heads(key_rows), by_heads(value_rows)])
    qkv_heads = lax.all_to_all(qkv, "dp", split_axis=2, concat_axis=1, tiled=True)

    projected = jnp.einsum(
        "te,kre->tkr", out_grad[0], weight, preferred_element_type=jnp.float32
    )
    grad_heads = lax.all_to_all(
        projected.astype(jnp.bfloat16), "dp", split_axis=1, concat_axis=0, tiled=True
    )
    total_rows = tok_rows * devices
    query_grad, key_grad, value_grad = attention_grads(
        qkv_heads[0].reshape(total_rows, HEAD_DIM),
        qkv_heads[1].reshape(total_rows, HEAD_DIM),
        qkv_heads[2].reshape(total_rows, HEAD_DIM),
        grad_heads.reshape(total_rows, HEAD_DIM),
        text_length,
    )
    grads = jnp.stack([query_grad, key_grad, value_grad]).reshape(3, devices, tok_rows, HEAD_DIM)
    returned = lax.all_to_all(grads, "dp", split_axis=1, concat_axis=1, tiled=True)
    returned = returned.transpose(0, 2, 1, 3).reshape(3, 1, tok_rows, HEADS * HEAD_DIM)
    return (returned[0], returned[1], returned[2])


def solution(mesh):
    in_specs = (
        P("seq", "dp", None),
        P("seq", "dp", None),
        P("seq", "dp", None),
        P("seq", "dp", None),
        P(None, ("dp", "seq"), None),
        P("seq"),
    )
    out_specs = (P("seq", "dp", None), P("seq", "dp", None), P("seq", "dp", None))
    return jax.shard_map(
        per_device, mesh=mesh, in_specs=in_specs, out_specs=out_specs, check_vma=False
    )
```

```python
import functools
import math

import jax
import jax.numpy as jnp
from jax import lax
from jax.experimental import pallas as pl
from jax.experimental.pallas import tpu as pltpu
from jax.sharding import PartitionSpec as P

HEADS = 16
HEAD_DIM = 128
TXT = 512
BLOCK_ROWS = 256


def attention_kernel(length_ref, q_ref, k_ref, v_ref, g_ref, dq_ref, dk_ref, dv_ref, dkt_acc, dvt_acc):
    step = pl.program_id(0)
    factor = 1.0 / math.sqrt(q_ref.shape[1])
    nt = (((1,), (1,)), ((), ()))

    @pl.when(step == 0)
    def _():
        dkt_acc[...] = jnp.zeros_like(dkt_acc)
        dvt_acc[...] = jnp.zeros_like(dvt_acc)

    query_block = q_ref[...]
    grad_block = g_ref[...]
    keys = k_ref[...]
    values = v_ref[...]
    scores = lax.dot_general(query_block, keys, nt, preferred_element_type=jnp.float32) * factor
    column = lax.broadcasted_iota(jnp.int32, scores.shape, 1)
    valid = (column >= TXT) | (column < length_ref[0])
    scores = jnp.where(valid, scores, -jnp.inf)
    shifted = jnp.exp(scores - jnp.max(scores, axis=1, keepdims=True))
    attention = shifted / jnp.sum(shifted, axis=1, keepdims=True)
    attention_low = attention.astype(jnp.bfloat16)
    grad_t = grad_block.astype(jnp.float32).T.astype(jnp.bfloat16)
    dvt_acc[...] += jnp.dot(grad_t, attention_low, preferred_element_type=jnp.float32)
    weight_grad = lax.dot_general(grad_block, values, nt, preferred_element_type=jnp.float32)
    row_dot = jnp.sum(attention * weight_grad, axis=1, keepdims=True)
    score_grad = (attention * (weight_grad - row_dot) * factor).astype(jnp.bfloat16)
    dq_ref[...] = jnp.dot(score_grad, keys, preferred_element_type=jnp.float32).astype(dq_ref.dtype)
    query_t = query_block.astype(jnp.float32).T.astype(jnp.bfloat16)
    dkt_acc[...] += jnp.dot(query_t, score_grad, preferred_element_type=jnp.float32)

    @pl.when(step == pl.num_programs(0) - 1)
    def _():
        dk_ref[...] = dkt_acc[...].T.astype(dk_ref.dtype)
        dv_ref[...] = dvt_acc[...].T.astype(dv_ref.dtype)


def attention_grads(query, key, value, grad, length):
    rows, width = query.shape
    block = min(BLOCK_ROWS, rows)
    row_spec = pl.BlockSpec((block, width), lambda i: (i, 0))
    full_spec = pl.BlockSpec((rows, width), lambda i: (0, 0))
    out = jax.ShapeDtypeStruct((rows, width), jnp.bfloat16)
    flops = 10 * rows * rows * width
    return pl.pallas_call(
        attention_kernel,
        grid=(rows // block,),
        in_specs=[
            pl.BlockSpec(memory_space=pltpu.SMEM),
            row_spec,
            full_spec,
            full_spec,
            row_spec,
        ],
        out_specs=[row_spec, full_spec, full_spec],
        out_shape=[out, out, out],
        scratch_shapes=[
            pltpu.VMEM((width, rows), jnp.float32),
            pltpu.VMEM((width, rows), jnp.float32),
        ],
        compiler_params=pltpu.CompilerParams(
            dimension_semantics=("arbitrary",), vmem_limit_bytes=48 * 1024 * 1024
        ),
        cost_estimate=pl.CostEstimate(
            flops=flops, transcendentals=rows * rows, bytes_accessed=7 * rows * width * 2
        ),
    )(length, query, key, value, grad)


def per_device(query_rows, key_rows, value_rows, out_grad, out_weight, text_length):
    devices = lax.axis_size("dp")
    tok_rows = query_rows.shape[1]

    def by_heads(array):
        return array[0].reshape(tok_rows, HEADS, HEAD_DIM)

    slot_text = (jnp.arange(devices) * tok_rows < TXT)[:, None, None]
    outgoing = jnp.where(slot_text, out_weight[0][None], out_weight[1][None])
    stream_rows = lax.all_to_all(outgoing, "dp", split_axis=0, concat_axis=0, tiled=True)

    ring = 4
    place = lax.axis_index("dp") % ring
    near_rows = stream_rows[:, : HEAD_DIM // 32 - 1]
    far_rows = lax.dynamic_slice_in_dim(
        stream_rows[:, HEAD_DIM // 32 - 1 :], place * (HEADS // ring), HEADS // ring, axis=0
    )
    far_gathered = lax.all_gather(far_rows, "seq", axis=0, tiled=False)
    near_rows, far_gathered = lax.optimization_barrier((near_rows, far_gathered))
    near_gathered = lax.all_gather(near_rows, "seq", axis=0, tiled=False)
    far_parts = [far_gathered]
    for shift in range(1, ring):
        pairs = [
            (row * ring + col, row * ring + (col + shift) % ring)
            for row in range(devices // ring)
            for col in range(ring)
        ]
        far_parts.append(lax.ppermute(far_gathered, "dp", pairs))
    far_parts = jnp.stack([far_parts[0]] + far_parts[:0:-1])

    qkv = jnp.stack([by_heads(query_rows), by_heads(key_rows), by_heads(value_rows)])
    qkv_heads = lax.all_to_all(qkv, "dp", split_axis=2, concat_axis=1, tiled=True)

    near_part = jnp.einsum(
        "te,qhre->thqr", out_grad[0], near_gathered, preferred_element_type=jnp.float32
    )
    far_part = jnp.einsum(
        "te,kqjre->tkjqr", out_grad[0], far_parts, preferred_element_type=jnp.float32
    )
    far_part = jnp.roll(far_part, place, axis=1).reshape(tok_rows, HEADS, -1, 1)
    projected = jnp.concatenate([near_part, far_part], axis=3).reshape(tok_rows, HEADS, HEAD_DIM)
    grad_heads = lax.all_to_all(
        projected.astype(jnp.bfloat16), "dp", split_axis=1, concat_axis=0, tiled=True
    )
    total_rows = tok_rows * devices
    query_grad, key_grad, value_grad = attention_grads(
        qkv_heads[0].reshape(total_rows, HEAD_DIM),
        qkv_heads[1].reshape(total_rows, HEAD_DIM),
        qkv_heads[2].reshape(total_rows, HEAD_DIM),
        grad_heads.reshape(total_rows, HEAD_DIM),
        text_length,
    )
    grads = jnp.stack([query_grad, key_grad, value_grad]).reshape(3, devices, tok_rows, HEAD_DIM)
    returned = lax.all_to_all(grads, "dp", split_axis=1, concat_axis=1, tiled=True)
    returned = returned.transpose(0, 2, 1, 3).reshape(3, 1, tok_rows, HEADS * HEAD_DIM)
    return (returned[0], returned[1], returned[2])


def solution(mesh):
    in_specs = (
        P("seq", "dp", None),
        P("seq", "dp", None),
        P("seq", "dp", None),
        P("seq", "dp", None),
        P(None, ("dp", "seq"), None),
        P("seq"),
    )
    out_specs = (P("seq", "dp", None), P("seq", "dp", None), P("seq", "dp", None))
    return jax.shard_map(
        per_device, mesh=mesh, in_specs=in_specs, out_specs=out_specs, check_vma=False
    )
```

```python
import functools
import math

import jax
import jax.numpy as jnp
from jax import lax
from jax.experimental import pallas as pl
from jax.experimental.pallas import tpu as pltpu
from jax.sharding import PartitionSpec as P

HEADS = 16
HEAD_DIM = 128
TXT = 512
BLOCK_ROWS = 256


def softmax_kernel(length_ref, q_ref, k_ref, p_ref):
    factor = 1.0 / math.sqrt(q_ref.shape[1])
    nt = (((1,), (1,)), ((), ()))
    scores = lax.dot_general(q_ref[...], k_ref[...], nt, preferred_element_type=jnp.float32) * factor
    column = lax.broadcasted_iota(jnp.int32, scores.shape, 1)
    valid = (column >= TXT) | (column < length_ref[0])
    scores = jnp.where(valid, scores, -jnp.inf)
    shifted = jnp.exp(scores - jnp.max(scores, axis=1, keepdims=True))
    p_ref[...] = shifted / jnp.sum(shifted, axis=1, keepdims=True)


def attention_probs(query, key, length):
    rows, width = query.shape
    block = min(BLOCK_ROWS, rows)
    return pl.pallas_call(
        softmax_kernel,
        grid=(rows // block,),
        in_specs=[
            pl.BlockSpec(memory_space=pltpu.SMEM),
            pl.BlockSpec((block, width), lambda i: (i, 0)),
            pl.BlockSpec((rows, width), lambda i: (0, 0)),
        ],
        out_specs=pl.BlockSpec((block, rows), lambda i: (i, 0)),
        out_shape=jax.ShapeDtypeStruct((rows, rows), jnp.float32),
        compiler_params=pltpu.CompilerParams(
            dimension_semantics=("arbitrary",), vmem_limit_bytes=48 * 1024 * 1024
        ),
        cost_estimate=pl.CostEstimate(
            flops=2 * rows * rows * width,
            transcendentals=rows * rows,
            bytes_accessed=2 * rows * width * 2 + rows * rows * 4,
        ),
    )(length, query, key)


def gradient_kernel(p_ref, q_ref, k_ref, v_ref, g_ref, dq_ref, dk_ref, dv_ref, dkt_acc, dvt_acc):
    step = pl.program_id(0)
    factor = 1.0 / math.sqrt(q_ref.shape[1])
    nt = (((1,), (1,)), ((), ()))

    @pl.when(step == 0)
    def _():
        dkt_acc[...] = jnp.zeros_like(dkt_acc)
        dvt_acc[...] = jnp.zeros_like(dvt_acc)

    attention = p_ref[...]
    grad_block = g_ref[...]
    keys = k_ref[...]
    attention_low = attention.astype(jnp.bfloat16)
    grad_t = grad_block.astype(jnp.float32).T.astype(jnp.bfloat16)
    dvt_acc[...] += jnp.dot(grad_t, attention_low, preferred_element_type=jnp.float32)
    weight_grad = lax.dot_general(grad_block, v_ref[...], nt, preferred_element_type=jnp.float32)
    row_dot = jnp.sum(attention * weight_grad, axis=1, keepdims=True)
    score_grad = (attention * (weight_grad - row_dot) * factor).astype(jnp.bfloat16)
    dq_ref[...] = jnp.dot(score_grad, keys, preferred_element_type=jnp.float32).astype(dq_ref.dtype)
    query_t = q_ref[...].astype(jnp.float32).T.astype(jnp.bfloat16)
    dkt_acc[...] += jnp.dot(query_t, score_grad, preferred_element_type=jnp.float32)

    @pl.when(step == pl.num_programs(0) - 1)
    def _():
        dk_ref[...] = dkt_acc[...].T.astype(dk_ref.dtype)
        dv_ref[...] = dvt_acc[...].T.astype(dv_ref.dtype)


def attention_grads(query, key, value, grad, length, probs=None):
    rows, width = query.shape
    if probs is None:
        probs = attention_probs(query, key, length)
    block = min(BLOCK_ROWS, rows)
    row_spec = pl.BlockSpec((block, width), lambda i: (i, 0))
    full_spec = pl.BlockSpec((rows, width), lambda i: (0, 0))
    out = jax.ShapeDtypeStruct((rows, width), jnp.bfloat16)
    return pl.pallas_call(
        gradient_kernel,
        grid=(rows // block,),
        in_specs=[
            pl.BlockSpec((block, rows), lambda i: (i, 0)),
            row_spec,
            full_spec,
            full_spec,
            row_spec,
        ],
        out_specs=[row_spec, full_spec, full_spec],
        out_shape=[out, out, out],
        scratch_shapes=[
            pltpu.VMEM((width, rows), jnp.float32),
            pltpu.VMEM((width, rows), jnp.float32),
        ],
        compiler_params=pltpu.CompilerParams(
            dimension_semantics=("arbitrary",), vmem_limit_bytes=48 * 1024 * 1024
        ),
        cost_estimate=pl.CostEstimate(
            flops=8 * rows * rows * width,
            transcendentals=0,
            bytes_accessed=7 * rows * width * 2 + rows * rows * 4,
        ),
    )(probs, query, key, value, grad)


def per_device(query_rows, key_rows, value_rows, out_grad, out_weight, text_length):
    devices = lax.axis_size("dp")
    tok_rows = query_rows.shape[1]

    def by_heads(array):
        return array[0].reshape(tok_rows, HEADS, HEAD_DIM)

    slot_text = (jnp.arange(devices) * tok_rows < TXT)[:, None, None]
    outgoing = jnp.where(slot_text, out_weight[0][None], out_weight[1][None])
    stream_rows = lax.all_to_all(outgoing, "dp", split_axis=0, concat_axis=0, tiled=True)
    weight = lax.all_gather(stream_rows, "seq", axis=1, tiled=True)

    qkv = jnp.stack([by_heads(query_rows), by_heads(key_rows), by_heads(value_rows)])
    qkv_heads = lax.all_to_all(qkv, "dp", split_axis=2, concat_axis=1, tiled=True)

    projected = jnp.einsum(
        "te,kre->tkr", out_grad[0], weight, preferred_element_type=jnp.float32
    )
    grad_heads = lax.all_to_all(
        projected.astype(jnp.bfloat16), "dp", split_axis=1, concat_axis=0, tiled=True
    )
    total_rows = tok_rows * devices
    query_heads = qkv_heads[0].reshape(total_rows, HEAD_DIM)
    key_heads = qkv_heads[1].reshape(total_rows, HEAD_DIM)
    probs = attention_probs(query_heads, key_heads, text_length)
    query_grad, key_grad, value_grad = attention_grads(
        query_heads,
        key_heads,
        qkv_heads[2].reshape(total_rows, HEAD_DIM),
        grad_heads.reshape(total_rows, HEAD_DIM),
        text_length,
        probs,
    )
    grads = jnp.stack([query_grad, key_grad, value_grad]).reshape(3, devices, tok_rows, HEAD_DIM)
    returned = lax.all_to_all(grads, "dp", split_axis=1, concat_axis=1, tiled=True)
    returned = returned.transpose(0, 2, 1, 3).reshape(3, 1, tok_rows, HEADS * HEAD_DIM)
    return (returned[0], returned[1], returned[2])


def solution(mesh):
    in_specs = (
        P("seq", "dp", None),
        P("seq", "dp", None),
        P("seq", "dp", None),
        P("seq", "dp", None),
        P(None, ("dp", "seq"), None),
        P("seq"),
    )
    out_specs = (P("seq", "dp", None), P("seq", "dp", None), P("seq", "dp", None))
    return jax.shard_map(
        per_device, mesh=mesh, in_specs=in_specs, out_specs=out_specs, check_vma=False
    )
```

```python
import functools
import math

import jax
import jax.numpy as jnp
from jax import lax
from jax.experimental import pallas as pl
from jax.experimental.pallas import tpu as pltpu
from jax.sharding import PartitionSpec as P

HEADS = 16
HEAD_DIM = 128
TXT = 512
BLOCK_ROWS = 256


def softmax_kernel(length_ref, q_ref, k_ref, p_ref):
    factor = 1.0 / math.sqrt(q_ref.shape[1])
    nt = (((1,), (1,)), ((), ()))
    scores = lax.dot_general(q_ref[...], k_ref[...], nt, preferred_element_type=jnp.float32) * factor
    column = lax.broadcasted_iota(jnp.int32, scores.shape, 1)
    valid = (column >= TXT) | (column < length_ref[0])
    scores = jnp.where(valid, scores, -jnp.inf)
    shifted = jnp.exp(scores - jnp.max(scores, axis=1, keepdims=True))
    p_ref[...] = shifted / jnp.sum(shifted, axis=1, keepdims=True)


def attention_probs(query, key, length):
    rows, width = query.shape
    block = min(BLOCK_ROWS, rows)
    return pl.pallas_call(
        softmax_kernel,
        grid=(rows // block,),
        in_specs=[
            pl.BlockSpec(memory_space=pltpu.SMEM),
            pl.BlockSpec((block, width), lambda i: (i, 0)),
            pl.BlockSpec((rows, width), lambda i: (0, 0)),
        ],
        out_specs=pl.BlockSpec((block, rows), lambda i: (i, 0)),
        out_shape=jax.ShapeDtypeStruct((rows, rows), jnp.float32),
        compiler_params=pltpu.CompilerParams(
            dimension_semantics=("arbitrary",), vmem_limit_bytes=48 * 1024 * 1024
        ),
        cost_estimate=pl.CostEstimate(
            flops=2 * rows * rows * width,
            transcendentals=rows * rows,
            bytes_accessed=2 * rows * width * 2 + rows * rows * 4,
        ),
    )(length, query, key)


def gradient_kernel(p_ref, q_ref, k_ref, v_ref, g_ref, dq_ref, dk_ref, dv_ref, dkt_acc, dvt_acc):
    step = pl.program_id(0)
    factor = 1.0 / math.sqrt(q_ref.shape[1])
    nt = (((1,), (1,)), ((), ()))

    @pl.when(step == 0)
    def _():
        dkt_acc[...] = jnp.zeros_like(dkt_acc)
        dvt_acc[...] = jnp.zeros_like(dvt_acc)

    attention = p_ref[...]
    grad_block = g_ref[...]
    keys = k_ref[...]
    attention_low = attention.astype(jnp.bfloat16)
    grad_t = grad_block.astype(jnp.float32).T.astype(jnp.bfloat16)
    dvt_acc[...] += jnp.dot(grad_t, attention_low, preferred_element_type=jnp.float32)
    weight_grad = lax.dot_general(grad_block, v_ref[...], nt, preferred_element_type=jnp.float32)
    row_dot = jnp.sum(attention * weight_grad, axis=1, keepdims=True)
    score_grad = (attention * (weight_grad - row_dot) * factor).astype(jnp.bfloat16)
    dq_ref[...] = jnp.dot(score_grad, keys, preferred_element_type=jnp.float32).astype(dq_ref.dtype)
    query_t = q_ref[...].astype(jnp.float32).T.astype(jnp.bfloat16)
    dkt_acc[...] += jnp.dot(query_t, score_grad, preferred_element_type=jnp.float32)

    @pl.when(step == pl.num_programs(0) - 1)
    def _():
        dk_ref[...] = dkt_acc[...].T.astype(dk_ref.dtype)
        dv_ref[...] = dvt_acc[...].T.astype(dv_ref.dtype)


def attention_grads(query, key, value, grad, length, probs=None):
    rows, width = query.shape
    if probs is None:
        probs = attention_probs(query, key, length)
    block = min(BLOCK_ROWS, rows)
    row_spec = pl.BlockSpec((block, width), lambda i: (i, 0))
    full_spec = pl.BlockSpec((rows, width), lambda i: (0, 0))
    out = jax.ShapeDtypeStruct((rows, width), jnp.bfloat16)
    return pl.pallas_call(
        gradient_kernel,
        grid=(rows // block,),
        in_specs=[
            pl.BlockSpec((block, rows), lambda i: (i, 0)),
            row_spec,
            full_spec,
            full_spec,
            row_spec,
        ],
        out_specs=[row_spec, full_spec, full_spec],
        out_shape=[out, out, out],
        scratch_shapes=[
            pltpu.VMEM((width, rows), jnp.float32),
            pltpu.VMEM((width, rows), jnp.float32),
        ],
        compiler_params=pltpu.CompilerParams(
            dimension_semantics=("arbitrary",), vmem_limit_bytes=48 * 1024 * 1024
        ),
        cost_estimate=pl.CostEstimate(
            flops=8 * rows * rows * width,
            transcendentals=0,
            bytes_accessed=7 * rows * width * 2 + rows * rows * 4,
        ),
    )(probs, query, key, value, grad)


def per_device(query_rows, key_rows, value_rows, out_grad, out_weight, text_length):
    devices = lax.axis_size("dp")
    tok_rows = query_rows.shape[1]

    def by_heads(array):
        return array[0].reshape(tok_rows, HEADS, HEAD_DIM)

    slot_text = (jnp.arange(devices) * tok_rows < TXT)[:, None, None]
    outgoing = jnp.where(slot_text, out_weight[0][None], out_weight[1][None])
    stream_rows = lax.all_to_all(outgoing, "dp", split_axis=0, concat_axis=0, tiled=True)

    ring = 4
    near = 2
    place = lax.axis_index("dp") % ring
    near_rows = stream_rows[:, :near]
    far_rows = lax.dynamic_slice_in_dim(
        stream_rows[:, near:], place * (HEADS // ring), HEADS // ring, axis=0
    )
    far_gathered = lax.all_gather(far_rows, "seq", axis=0, tiled=False)
    near_rows, far_gathered = lax.optimization_barrier((near_rows, far_gathered))
    near_gathered = lax.all_gather(near_rows, "seq", axis=0, tiled=False)
    far_parts = [far_gathered]
    for shift in range(1, ring):
        pairs = [
            (row * ring + col, row * ring + (col + shift) % ring)
            for row in range(devices // ring)
            for col in range(ring)
        ]
        far_parts.append(lax.ppermute(far_gathered, "dp", pairs))
    far_parts = jnp.stack([far_parts[0]] + far_parts[:0:-1])

    qkv = jnp.stack([by_heads(query_rows), by_heads(key_rows), by_heads(value_rows)])
    qkv_heads = lax.all_to_all(qkv, "dp", split_axis=2, concat_axis=1, tiled=True)

    near_part = jnp.einsum(
        "te,qhre->thqr", out_grad[0], near_gathered, preferred_element_type=jnp.float32
    )
    far_part = jnp.einsum(
        "te,kqjre->tkjqr", out_grad[0], far_parts, preferred_element_type=jnp.float32
    )
    far_part = jnp.roll(far_part, place, axis=1).reshape(tok_rows, HEADS, far_part.shape[3], -1)
    projected = jnp.concatenate([near_part, far_part], axis=3).reshape(tok_rows, HEADS, HEAD_DIM)
    grad_heads = lax.all_to_all(
        projected.astype(jnp.bfloat16), "dp", split_axis=1, concat_axis=0, tiled=True
    )
    total_rows = tok_rows * devices
    query_heads = qkv_heads[0].reshape(total_rows, HEAD_DIM)
    key_heads = qkv_heads[1].reshape(total_rows, HEAD_DIM)
    probs = attention_probs(query_heads, key_heads, text_length)
    query_grad, key_grad, value_grad = attention_grads(
        query_heads,
        key_heads,
        qkv_heads[2].reshape(total_rows, HEAD_DIM),
        grad_heads.reshape(total_rows, HEAD_DIM),
        text_length,
        probs,
    )
    grads = jnp.stack([query_grad, key_grad, value_grad]).reshape(3, devices, tok_rows, HEAD_DIM)
    returned = lax.all_to_all(grads, "dp", split_axis=1, concat_axis=1, tiled=True)
    returned = returned.transpose(0, 2, 1, 3).reshape(3, 1, tok_rows, HEADS * HEAD_DIM)
    return (returned[0], returned[1], returned[2])


def solution(mesh):
    in_specs = (
        P("seq", "dp", None),
        P("seq", "dp", None),
        P("seq", "dp", None),
        P("seq", "dp", None),
        P(None, ("dp", "seq"), None),
        P("seq"),
    )
    out_specs = (P("seq", "dp", None), P("seq", "dp", None), P("seq", "dp", None))
    return jax.shard_map(
        per_device, mesh=mesh, in_specs=in_specs, out_specs=out_specs, check_vma=False
    )
```

```python
import functools
import math

import jax
import jax.numpy as jnp
from jax import lax
from jax.experimental import pallas as pl
from jax.experimental.pallas import tpu as pltpu
from jax.sharding import PartitionSpec as P

HEADS = 16
HEAD_DIM = 128
TXT = 512
BLOCK_ROWS = 256


def softmax_kernel(length_ref, q_ref, k_ref, p_ref):
    factor = 1.0 / math.sqrt(q_ref.shape[1])
    nt = (((1,), (1,)), ((), ()))
    scores = lax.dot_general(q_ref[...], k_ref[...], nt, preferred_element_type=jnp.float32) * factor
    column = lax.broadcasted_iota(jnp.int32, scores.shape, 1)
    valid = (column >= TXT) | (column < length_ref[0])
    scores = jnp.where(valid, scores, -jnp.inf)
    shifted = jnp.exp(scores - jnp.max(scores, axis=1, keepdims=True))
    p_ref[...] = shifted / jnp.sum(shifted, axis=1, keepdims=True)


def attention_probs(query, key, length):
    rows, width = query.shape
    block = min(BLOCK_ROWS, rows)
    return pl.pallas_call(
        softmax_kernel,
        grid=(rows // block,),
        in_specs=[
            pl.BlockSpec(memory_space=pltpu.SMEM),
            pl.BlockSpec((block, width), lambda i: (i, 0)),
            pl.BlockSpec((rows, width), lambda i: (0, 0)),
        ],
        out_specs=pl.BlockSpec((block, rows), lambda i: (i, 0)),
        out_shape=jax.ShapeDtypeStruct((rows, rows), jnp.float32),
        compiler_params=pltpu.CompilerParams(
            dimension_semantics=("arbitrary",), vmem_limit_bytes=48 * 1024 * 1024
        ),
        cost_estimate=pl.CostEstimate(
            flops=2 * rows * rows * width,
            transcendentals=rows * rows,
            bytes_accessed=2 * rows * width * 2 + rows * rows * 4,
        ),
    )(length, query, key)


def query_grad_kernel(p_ref, k_ref, v_ref, g_ref, dq_ref):
    factor = 1.0 / math.sqrt(k_ref.shape[1])
    nt = (((1,), (1,)), ((), ()))
    attention = p_ref[...]
    weight_grad = lax.dot_general(g_ref[...], v_ref[...], nt, preferred_element_type=jnp.float32)
    row_dot = jnp.sum(attention * weight_grad, axis=1, keepdims=True)
    score_grad = (attention * (weight_grad - row_dot) * factor).astype(jnp.bfloat16)
    dq_ref[...] = jnp.dot(score_grad, k_ref[...], preferred_element_type=jnp.float32).astype(
        dq_ref.dtype
    )


def key_value_grad_kernel(p_ref, q_ref, v_ref, g_ref, dk_ref, dv_ref, dkt_acc, dvt_acc):
    step = pl.program_id(0)
    factor = 1.0 / math.sqrt(q_ref.shape[1])
    nt = (((1,), (1,)), ((), ()))

    @pl.when(step == 0)
    def _():
        dkt_acc[...] = jnp.zeros_like(dkt_acc)
        dvt_acc[...] = jnp.zeros_like(dvt_acc)

    attention = p_ref[...]
    grad_block = g_ref[...]
    attention_low = attention.astype(jnp.bfloat16)
    grad_t = grad_block.astype(jnp.float32).T.astype(jnp.bfloat16)
    dvt_acc[...] += jnp.dot(grad_t, attention_low, preferred_element_type=jnp.float32)
    weight_grad = lax.dot_general(grad_block, v_ref[...], nt, preferred_element_type=jnp.float32)
    row_dot = jnp.sum(attention * weight_grad, axis=1, keepdims=True)
    score_grad = (attention * (weight_grad - row_dot) * factor).astype(jnp.bfloat16)
    query_t = q_ref[...].astype(jnp.float32).T.astype(jnp.bfloat16)
    dkt_acc[...] += jnp.dot(query_t, score_grad, preferred_element_type=jnp.float32)

    @pl.when(step == pl.num_programs(0) - 1)
    def _():
        dk_ref[...] = dkt_acc[...].T.astype(dk_ref.dtype)
        dv_ref[...] = dvt_acc[...].T.astype(dv_ref.dtype)


def _params():
    return pltpu.CompilerParams(dimension_semantics=("arbitrary",), vmem_limit_bytes=48 * 1024 * 1024)


def query_grads(probs, key, value, grad):
    rows, width = key.shape
    block = min(BLOCK_ROWS, rows)
    row_spec = pl.BlockSpec((block, width), lambda i: (i, 0))
    full_spec = pl.BlockSpec((rows, width), lambda i: (0, 0))
    return pl.pallas_call(
        query_grad_kernel,
        grid=(rows // block,),
        in_specs=[pl.BlockSpec((block, rows), lambda i: (i, 0)), full_spec, full_spec, row_spec],
        out_specs=row_spec,
        out_shape=jax.ShapeDtypeStruct((rows, width), jnp.bfloat16),
        compiler_params=_params(),
        cost_estimate=pl.CostEstimate(
            flops=4 * rows * rows * width,
            transcendentals=0,
            bytes_accessed=4 * rows * width * 2 + rows * rows * 4,
        ),
    )(probs, key, value, grad)


def key_value_grads(probs, query, value, grad):
    rows, width = query.shape
    block = min(BLOCK_ROWS, rows)
    row_spec = pl.BlockSpec((block, width), lambda i: (i, 0))
    full_spec = pl.BlockSpec((rows, width), lambda i: (0, 0))
    out = jax.ShapeDtypeStruct((rows, width), jnp.bfloat16)
    return pl.pallas_call(
        key_value_grad_kernel,
        grid=(rows // block,),
        in_specs=[pl.BlockSpec((block, rows), lambda i: (i, 0)), row_spec, full_spec, row_spec],
        out_specs=[full_spec, full_spec],
        out_shape=[out, out],
        scratch_shapes=[
            pltpu.VMEM((width, rows), jnp.float32),
            pltpu.VMEM((width, rows), jnp.float32),
        ],
        compiler_params=_params(),
        cost_estimate=pl.CostEstimate(
            flops=6 * rows * rows * width,
            transcendentals=0,
            bytes_accessed=5 * rows * width * 2 + rows * rows * 4,
        ),
    )(probs, query, value, grad)


def attention_grads(query, key, value, grad, length, probs=None):
    if probs is None:
        probs = attention_probs(query, key, length)
    key_grad, value_grad = key_value_grads(probs, query, value, grad)
    return (query_grads(probs, key, value, grad), key_grad, value_grad)


def per_device(query_rows, key_rows, value_rows, out_grad, out_weight, text_length):
    devices = lax.axis_size("dp")
    tok_rows = query_rows.shape[1]

    def by_heads(array):
        return array[0].reshape(tok_rows, HEADS, HEAD_DIM)

    slot_text = (jnp.arange(devices) * tok_rows < TXT)[:, None, None]
    outgoing = jnp.where(slot_text, out_weight[0][None], out_weight[1][None])
    stream_rows = lax.all_to_all(outgoing, "dp", split_axis=0, concat_axis=0, tiled=True)
    weight = lax.all_gather(stream_rows, "seq", axis=1, tiled=True)

    qkv = jnp.stack([by_heads(query_rows), by_heads(key_rows), by_heads(value_rows)])
    qkv_heads = lax.all_to_all(qkv, "dp", split_axis=2, concat_axis=1, tiled=True)

    projected = jnp.einsum(
        "te,kre->tkr", out_grad[0], weight, preferred_element_type=jnp.float32
    )
    grad_heads = lax.all_to_all(
        projected.astype(jnp.bfloat16), "dp", split_axis=1, concat_axis=0, tiled=True
    )
    total_rows = tok_rows * devices
    query_heads = qkv_heads[0].reshape(total_rows, HEAD_DIM)
    key_heads = qkv_heads[1].reshape(total_rows, HEAD_DIM)
    value_heads = qkv_heads[2].reshape(total_rows, HEAD_DIM)
    grad_heads = grad_heads.reshape(total_rows, HEAD_DIM)
    probs = attention_probs(query_heads, key_heads, text_length)

    def send_back(grads):
        count = len(grads)
        stacked = jnp.stack(grads).reshape(count, devices, tok_rows, HEAD_DIM)
        returned = lax.all_to_all(stacked, "dp", split_axis=1, concat_axis=1, tiled=True)
        return returned.transpose(0, 2, 1, 3).reshape(count, 1, tok_rows, HEADS * HEAD_DIM)

    query_back = send_back([query_grads(probs, key_heads, value_heads, grad_heads)])
    key_value_back = send_back(list(key_value_grads(probs, query_heads, value_heads, grad_heads)))
    return (query_back[0], key_value_back[0], key_value_back[1])


def solution(mesh):
    in_specs = (
        P("seq", "dp", None),
        P("seq", "dp", None),
        P("seq", "dp", None),
        P("seq", "dp", None),
        P(None, ("dp", "seq"), None),
        P("seq"),
    )
    out_specs = (P("seq", "dp", None), P("seq", "dp", None), P("seq", "dp", None))
    return jax.shard_map(
        per_device, mesh=mesh, in_specs=in_specs, out_specs=out_specs, check_vma=False
    )
```

```python
import functools
import math

import jax
import jax.numpy as jnp
from jax import lax
from jax.experimental import pallas as pl
from jax.experimental.pallas import tpu as pltpu
from jax.sharding import PartitionSpec as P

HEADS = 16
HEAD_DIM = 128
TXT = 512
BLOCK_ROWS = 256


def softmax_kernel(length_ref, q_ref, k_ref, p_ref):
    factor = 1.0 / math.sqrt(q_ref.shape[1])
    nt = (((1,), (1,)), ((), ()))
    scores = lax.dot_general(q_ref[...], k_ref[...], nt, preferred_element_type=jnp.float32) * factor
    column = lax.broadcasted_iota(jnp.int32, scores.shape, 1)
    valid = (column >= TXT) | (column < length_ref[0])
    scores = jnp.where(valid, scores, -jnp.inf)
    shifted = jnp.exp(scores - jnp.max(scores, axis=1, keepdims=True))
    p_ref[...] = shifted / jnp.sum(shifted, axis=1, keepdims=True)


def attention_probs(query, key, length):
    rows, width = query.shape
    block = min(BLOCK_ROWS, rows)
    return pl.pallas_call(
        softmax_kernel,
        grid=(rows // block,),
        in_specs=[
            pl.BlockSpec(memory_space=pltpu.SMEM),
            pl.BlockSpec((block, width), lambda i: (i, 0)),
            pl.BlockSpec((rows, width), lambda i: (0, 0)),
        ],
        out_specs=pl.BlockSpec((block, rows), lambda i: (i, 0)),
        out_shape=jax.ShapeDtypeStruct((rows, rows), jnp.float32),
        compiler_params=pltpu.CompilerParams(
            dimension_semantics=("arbitrary",), vmem_limit_bytes=48 * 1024 * 1024
        ),
        cost_estimate=pl.CostEstimate(
            flops=2 * rows * rows * width,
            transcendentals=rows * rows,
            bytes_accessed=2 * rows * width * 2 + rows * rows * 4,
        ),
    )(length, query, key)


def gradient_kernel(p_ref, q_ref, k_ref, v_ref, g_ref, dq_ref, dk_ref, dv_ref, dkt_acc, dvt_acc):
    step = pl.program_id(0)
    factor = 1.0 / math.sqrt(q_ref.shape[1])
    nt = (((1,), (1,)), ((), ()))

    @pl.when(step == 0)
    def _():
        dkt_acc[...] = jnp.zeros_like(dkt_acc)
        dvt_acc[...] = jnp.zeros_like(dvt_acc)

    attention = p_ref[...]
    grad_block = g_ref[...]
    keys = k_ref[...]
    attention_low = attention.astype(jnp.bfloat16)
    grad_t = grad_block.astype(jnp.float32).T.astype(jnp.bfloat16)
    dvt_acc[...] += jnp.dot(grad_t, attention_low, preferred_element_type=jnp.float32)
    weight_grad = lax.dot_general(grad_block, v_ref[...], nt, preferred_element_type=jnp.float32)
    row_dot = jnp.sum(attention * weight_grad, axis=1, keepdims=True)
    score_grad = (attention * (weight_grad - row_dot) * factor).astype(jnp.bfloat16)
    dq_ref[...] = jnp.dot(score_grad, keys, preferred_element_type=jnp.float32).astype(dq_ref.dtype)
    query_t = q_ref[...].astype(jnp.float32).T.astype(jnp.bfloat16)
    dkt_acc[...] += jnp.dot(query_t, score_grad, preferred_element_type=jnp.float32)

    @pl.when(step == pl.num_programs(0) - 1)
    def _():
        dk_ref[...] = dkt_acc[...].T.astype(dk_ref.dtype)
        dv_ref[...] = dvt_acc[...].T.astype(dv_ref.dtype)


def attention_grads(query, key, value, grad, length, probs=None):
    rows, width = query.shape
    if probs is None:
        probs = attention_probs(query, key, length)
    block = min(BLOCK_ROWS, rows)
    row_spec = pl.BlockSpec((block, width), lambda i: (i, 0))
    full_spec = pl.BlockSpec((rows, width), lambda i: (0, 0))
    out = jax.ShapeDtypeStruct((rows, width), jnp.bfloat16)
    return pl.pallas_call(
        gradient_kernel,
        grid=(rows // block,),
        in_specs=[
            pl.BlockSpec((block, rows), lambda i: (i, 0)),
            row_spec,
            full_spec,
            full_spec,
            row_spec,
        ],
        out_specs=[row_spec, full_spec, full_spec],
        out_shape=[out, out, out],
        scratch_shapes=[
            pltpu.VMEM((width, rows), jnp.float32),
            pltpu.VMEM((width, rows), jnp.float32),
        ],
        compiler_params=pltpu.CompilerParams(
            dimension_semantics=("arbitrary",), vmem_limit_bytes=48 * 1024 * 1024
        ),
        cost_estimate=pl.CostEstimate(
            flops=8 * rows * rows * width,
            transcendentals=0,
            bytes_accessed=7 * rows * width * 2 + rows * rows * 4,
        ),
    )(probs, query, key, value, grad)


def relayout_kernel(block_ref, *out_refs):
    for index, out_ref in enumerate(out_refs):
        out_ref[...] = block_ref[0, index]


def relayout(blocks):
    heads, count, rows, width = blocks.shape
    return pl.pallas_call(
        relayout_kernel,
        grid=(heads,),
        in_specs=[pl.BlockSpec((1, count, rows, width), lambda h: (h, 0, 0, 0))],
        out_specs=[pl.BlockSpec((rows, width), lambda h: (0, h))] * count,
        out_shape=[jax.ShapeDtypeStruct((rows, heads * width), blocks.dtype)] * count,
        compiler_params=pltpu.CompilerParams(dimension_semantics=("arbitrary",)),
        cost_estimate=pl.CostEstimate(
            flops=0, transcendentals=0, bytes_accessed=2 * blocks.size * blocks.dtype.itemsize
        ),
    )(blocks)


def per_device(query_rows, key_rows, value_rows, out_grad, out_weight, text_length):
    devices = lax.axis_size("dp")
    tok_rows = query_rows.shape[1]

    def by_heads(array):
        return array[0].reshape(tok_rows, HEADS, HEAD_DIM)

    slot_text = (jnp.arange(devices) * tok_rows < TXT)[:, None, None]
    outgoing = jnp.where(slot_text, out_weight[0][None], out_weight[1][None])
    stream_rows = lax.all_to_all(outgoing, "dp", split_axis=0, concat_axis=0, tiled=True)
    weight = lax.all_gather(stream_rows, "seq", axis=1, tiled=True)

    qkv = jnp.stack([by_heads(query_rows), by_heads(key_rows), by_heads(value_rows)])
    qkv_heads = lax.all_to_all(qkv, "dp", split_axis=2, concat_axis=1, tiled=True)

    projected = jnp.einsum(
        "te,kre->tkr", out_grad[0], weight, preferred_element_type=jnp.float32
    )
    grad_heads = lax.all_to_all(
        projected.astype(jnp.bfloat16), "dp", split_axis=1, concat_axis=0, tiled=True
    )
    total_rows = tok_rows * devices
    query_heads = qkv_heads[0].reshape(total_rows, HEAD_DIM)
    key_heads = qkv_heads[1].reshape(total_rows, HEAD_DIM)
    probs = attention_probs(query_heads, key_heads, text_length)
    query_grad, key_grad, value_grad = attention_grads(
        query_heads,
        key_heads,
        qkv_heads[2].reshape(total_rows, HEAD_DIM),
        grad_heads.reshape(total_rows, HEAD_DIM),
        text_length,
        probs,
    )
    grads = jnp.stack([query_grad, key_grad, value_grad]).reshape(3, devices, tok_rows, HEAD_DIM)
    returned = lax.all_to_all(grads.transpose(1, 0, 2, 3), "dp", split_axis=0, concat_axis=0, tiled=True)
    return tuple(out.reshape(1, tok_rows, HEADS * HEAD_DIM) for out in relayout(returned))


def solution(mesh):
    in_specs = (
        P("seq", "dp", None),
        P("seq", "dp", None),
        P("seq", "dp", None),
        P("seq", "dp", None),
        P(None, ("dp", "seq"), None),
        P("seq"),
    )
    out_specs = (P("seq", "dp", None), P("seq", "dp", None), P("seq", "dp", None))
    return jax.shard_map(
        per_device, mesh=mesh, in_specs=in_specs, out_specs=out_specs, check_vma=False
    )
```

```python
import functools
import math

import jax
import jax.numpy as jnp
from jax import lax
from jax.experimental import pallas as pl
from jax.experimental.pallas import tpu as pltpu
from jax.sharding import PartitionSpec as P

HEADS = 16
HEAD_DIM = 128
TXT = 512
BLOCK_ROWS = 256


def softmax_kernel(length_ref, q_ref, k_ref, p_ref):
    factor = 1.0 / math.sqrt(q_ref.shape[1])
    nt = (((1,), (1,)), ((), ()))
    scores = lax.dot_general(q_ref[...], k_ref[...], nt, preferred_element_type=jnp.float32) * factor
    column = lax.broadcasted_iota(jnp.int32, scores.shape, 1)
    valid = (column >= TXT) | (column < length_ref[0])
    scores = jnp.where(valid, scores, -jnp.inf)
    shifted = jnp.exp(scores - jnp.max(scores, axis=1, keepdims=True))
    p_ref[...] = shifted / jnp.sum(shifted, axis=1, keepdims=True)


def attention_probs(query, key, length):
    rows, width = query.shape
    block = min(BLOCK_ROWS, rows)
    return pl.pallas_call(
        softmax_kernel,
        grid=(rows // block,),
        in_specs=[
            pl.BlockSpec(memory_space=pltpu.SMEM),
            pl.BlockSpec((block, width), lambda i: (i, 0)),
            pl.BlockSpec((rows, width), lambda i: (0, 0)),
        ],
        out_specs=pl.BlockSpec((block, rows), lambda i: (i, 0)),
        out_shape=jax.ShapeDtypeStruct((rows, rows), jnp.float32),
        compiler_params=pltpu.CompilerParams(
            dimension_semantics=("arbitrary",), vmem_limit_bytes=48 * 1024 * 1024
        ),
        cost_estimate=pl.CostEstimate(
            flops=2 * rows * rows * width,
            transcendentals=rows * rows,
            bytes_accessed=2 * rows * width * 2 + rows * rows * 4,
        ),
    )(length, query, key)


def gradient_kernel(p_ref, q_ref, k_ref, v_ref, g_ref, dq_ref, dk_ref, dv_ref, dkt_acc, dvt_acc):
    step = pl.program_id(0)
    factor = 1.0 / math.sqrt(q_ref.shape[1])
    nt = (((1,), (1,)), ((), ()))

    @pl.when(step == 0)
    def _():
        dkt_acc[...] = jnp.zeros_like(dkt_acc)
        dvt_acc[...] = jnp.zeros_like(dvt_acc)

    attention = p_ref[...]
    grad_block = g_ref[...]
    keys = k_ref[...]
    attention_low = attention.astype(jnp.bfloat16)
    grad_t = grad_block.astype(jnp.float32).T.astype(jnp.bfloat16)
    dvt_acc[...] += jnp.dot(grad_t, attention_low, preferred_element_type=jnp.float32)
    weight_grad = lax.dot_general(grad_block, v_ref[...], nt, preferred_element_type=jnp.float32)
    row_dot = jnp.sum(attention * weight_grad, axis=1, keepdims=True)
    score_grad = (attention * (weight_grad - row_dot) * factor).astype(jnp.bfloat16)
    dq_ref[...] = jnp.dot(score_grad, keys, preferred_element_type=jnp.float32).astype(dq_ref.dtype)
    query_t = q_ref[...].astype(jnp.float32).T.astype(jnp.bfloat16)
    dkt_acc[...] += jnp.dot(query_t, score_grad, preferred_element_type=jnp.float32)

    @pl.when(step == pl.num_programs(0) - 1)
    def _():
        dk_ref[...] = dkt_acc[...].T.astype(dk_ref.dtype)
        dv_ref[...] = dvt_acc[...].T.astype(dv_ref.dtype)


def attention_grads(query, key, value, grad, length, probs=None):
    rows, width = query.shape
    if probs is None:
        probs = attention_probs(query, key, length)
    block = min(BLOCK_ROWS, rows)
    row_spec = pl.BlockSpec((block, width), lambda i: (i, 0))
    full_spec = pl.BlockSpec((rows, width), lambda i: (0, 0))
    out = jax.ShapeDtypeStruct((rows, width), jnp.bfloat16)
    return pl.pallas_call(
        gradient_kernel,
        grid=(rows // block,),
        in_specs=[
            pl.BlockSpec((block, rows), lambda i: (i, 0)),
            row_spec,
            full_spec,
            full_spec,
            row_spec,
        ],
        out_specs=[row_spec, full_spec, full_spec],
        out_shape=[out, out, out],
        scratch_shapes=[
            pltpu.VMEM((width, rows), jnp.float32),
            pltpu.VMEM((width, rows), jnp.float32),
        ],
        compiler_params=pltpu.CompilerParams(
            dimension_semantics=("arbitrary",), vmem_limit_bytes=48 * 1024 * 1024
        ),
        cost_estimate=pl.CostEstimate(
            flops=8 * rows * rows * width,
            transcendentals=0,
            bytes_accessed=7 * rows * width * 2 + rows * rows * 4,
        ),
    )(probs, query, key, value, grad)


def relayout_kernel(block_ref, *out_refs):
    heads, _, _, width = block_ref.shape
    for index, out_ref in enumerate(out_refs):
        for head in range(heads):
            out_ref[:, head * width : (head + 1) * width] = block_ref[head, index]


def relayout(blocks):
    heads, count, rows, width = blocks.shape
    return pl.pallas_call(
        relayout_kernel,
        in_specs=[pl.BlockSpec(memory_space=pltpu.VMEM)],
        out_specs=[pl.BlockSpec(memory_space=pltpu.VMEM)] * count,
        out_shape=[jax.ShapeDtypeStruct((rows, heads * width), blocks.dtype)] * count,
        cost_estimate=pl.CostEstimate(
            flops=0, transcendentals=0, bytes_accessed=2 * blocks.size * blocks.dtype.itemsize
        ),
    )(blocks)


def per_device(query_rows, key_rows, value_rows, out_grad, out_weight, text_length):
    devices = lax.axis_size("dp")
    tok_rows = query_rows.shape[1]

    def by_heads(array):
        return array[0].reshape(tok_rows, HEADS, HEAD_DIM)

    slot_text = (jnp.arange(devices) * tok_rows < TXT)[:, None, None]
    outgoing = jnp.where(slot_text, out_weight[0][None], out_weight[1][None])
    stream_rows = lax.all_to_all(outgoing, "dp", split_axis=0, concat_axis=0, tiled=True)
    weight = lax.all_gather(stream_rows, "seq", axis=1, tiled=True)

    qkv = jnp.stack([by_heads(query_rows), by_heads(key_rows), by_heads(value_rows)])
    qkv_heads = lax.all_to_all(qkv, "dp", split_axis=2, concat_axis=1, tiled=True)

    projected = jnp.einsum(
        "te,kre->tkr", out_grad[0], weight, preferred_element_type=jnp.float32
    )
    grad_heads = lax.all_to_all(
        projected.astype(jnp.bfloat16), "dp", split_axis=1, concat_axis=0, tiled=True
    )
    total_rows = tok_rows * devices
    query_heads = qkv_heads[0].reshape(total_rows, HEAD_DIM)
    key_heads = qkv_heads[1].reshape(total_rows, HEAD_DIM)
    probs = attention_probs(query_heads, key_heads, text_length)
    query_grad, key_grad, value_grad = attention_grads(
        query_heads,
        key_heads,
        qkv_heads[2].reshape(total_rows, HEAD_DIM),
        grad_heads.reshape(total_rows, HEAD_DIM),
        text_length,
        probs,
    )
    grads = jnp.stack([query_grad, key_grad, value_grad]).reshape(3, devices, tok_rows, HEAD_DIM)
    returned = lax.all_to_all(grads.transpose(1, 0, 2, 3), "dp", split_axis=0, concat_axis=0, tiled=True)
    return tuple(out.reshape(1, tok_rows, HEADS * HEAD_DIM) for out in relayout(returned))


def solution(mesh):
    in_specs = (
        P("seq", "dp", None),
        P("seq", "dp", None),
        P("seq", "dp", None),
        P("seq", "dp", None),
        P(None, ("dp", "seq"), None),
        P("seq"),
    )
    out_specs = (P("seq", "dp", None), P("seq", "dp", None), P("seq", "dp", None))
    return jax.shard_map(
        per_device, mesh=mesh, in_specs=in_specs, out_specs=out_specs, check_vma=False
    )
```

```python
import functools
import math

import jax
import jax.numpy as jnp
from jax import lax
from jax.experimental import pallas as pl
from jax.experimental.pallas import tpu as pltpu
from jax.sharding import Mesh, PartitionSpec as P

HEADS = 16
HEAD_DIM = 128
TXT = 512
BLOCK_ROWS = 256


def softmax_kernel(length_ref, q_ref, k_ref, p_ref):
    factor = 1.0 / math.sqrt(q_ref.shape[1])
    nt = (((1,), (1,)), ((), ()))
    scores = lax.dot_general(q_ref[...], k_ref[...], nt, preferred_element_type=jnp.float32) * factor
    column = lax.broadcasted_iota(jnp.int32, scores.shape, 1)
    valid = (column >= TXT) | (column < length_ref[0])
    scores = jnp.where(valid, scores, -jnp.inf)
    shifted = jnp.exp(scores - jnp.max(scores, axis=1, keepdims=True))
    p_ref[...] = shifted / jnp.sum(shifted, axis=1, keepdims=True)


def attention_probs(query, key, length):
    rows, width = query.shape
    block = min(BLOCK_ROWS, rows)
    return pl.pallas_call(
        softmax_kernel,
        grid=(rows // block,),
        in_specs=[
            pl.BlockSpec(memory_space=pltpu.SMEM),
            pl.BlockSpec((block, width), lambda i: (i, 0)),
            pl.BlockSpec((rows, width), lambda i: (0, 0)),
        ],
        out_specs=pl.BlockSpec((block, rows), lambda i: (i, 0)),
        out_shape=jax.ShapeDtypeStruct((rows, rows), jnp.float32),
        compiler_params=pltpu.CompilerParams(
            dimension_semantics=("arbitrary",), vmem_limit_bytes=48 * 1024 * 1024
        ),
        cost_estimate=pl.CostEstimate(
            flops=2 * rows * rows * width,
            transcendentals=rows * rows,
            bytes_accessed=2 * rows * width * 2 + rows * rows * 4,
        ),
    )(length, query, key)


def gradient_kernel(p_ref, q_ref, k_ref, v_ref, g_ref, dq_ref, dk_ref, dv_ref, dkt_acc, dvt_acc):
    step = pl.program_id(0)
    factor = 1.0 / math.sqrt(q_ref.shape[1])
    nt = (((1,), (1,)), ((), ()))

    @pl.when(step == 0)
    def _():
        dkt_acc[...] = jnp.zeros_like(dkt_acc)
        dvt_acc[...] = jnp.zeros_like(dvt_acc)

    attention = p_ref[...]
    grad_block = g_ref[...]
    keys = k_ref[...]
    attention_low = attention.astype(jnp.bfloat16)
    grad_t = grad_block.astype(jnp.float32).T.astype(jnp.bfloat16)
    dvt_acc[...] += jnp.dot(grad_t, attention_low, preferred_element_type=jnp.float32)
    weight_grad = lax.dot_general(grad_block, v_ref[...], nt, preferred_element_type=jnp.float32)
    row_dot = jnp.sum(attention * weight_grad, axis=1, keepdims=True)
    score_grad = (attention * (weight_grad - row_dot) * factor).astype(jnp.bfloat16)
    dq_ref[...] = jnp.dot(score_grad, keys, preferred_element_type=jnp.float32).astype(dq_ref.dtype)
    query_t = q_ref[...].astype(jnp.float32).T.astype(jnp.bfloat16)
    dkt_acc[...] += jnp.dot(query_t, score_grad, preferred_element_type=jnp.float32)

    @pl.when(step == pl.num_programs(0) - 1)
    def _():
        dk_ref[...] = dkt_acc[...].T.astype(dk_ref.dtype)
        dv_ref[...] = dvt_acc[...].T.astype(dv_ref.dtype)


def attention_grads(query, key, value, grad, length, probs=None):
    rows, width = query.shape
    if probs is None:
        probs = attention_probs(query, key, length)
    block = min(BLOCK_ROWS, rows)
    row_spec = pl.BlockSpec((block, width), lambda i: (i, 0))
    full_spec = pl.BlockSpec((rows, width), lambda i: (0, 0))
    out = jax.ShapeDtypeStruct((rows, width), jnp.bfloat16)
    return pl.pallas_call(
        gradient_kernel,
        grid=(rows // block,),
        in_specs=[
            pl.BlockSpec((block, rows), lambda i: (i, 0)),
            row_spec,
            full_spec,
            full_spec,
            row_spec,
        ],
        out_specs=[row_spec, full_spec, full_spec],
        out_shape=[out, out, out],
        scratch_shapes=[
            pltpu.VMEM((width, rows), jnp.float32),
            pltpu.VMEM((width, rows), jnp.float32),
        ],
        compiler_params=pltpu.CompilerParams(
            dimension_semantics=("arbitrary",), vmem_limit_bytes=48 * 1024 * 1024
        ),
        cost_estimate=pl.CostEstimate(
            flops=8 * rows * rows * width,
            transcendentals=0,
            bytes_accessed=7 * rows * width * 2 + rows * rows * 4,
        ),
    )(probs, query, key, value, grad)


def relayout_kernel(block_ref, *out_refs):
    heads, _, _, width = block_ref.shape
    for index, out_ref in enumerate(out_refs):
        for head in range(heads):
            out_ref[:, head * width : (head + 1) * width] = block_ref[head, index]


def relayout(blocks):
    heads, count, rows, width = blocks.shape
    return pl.pallas_call(
        relayout_kernel,
        in_specs=[pl.BlockSpec(memory_space=pltpu.VMEM)],
        out_specs=[pl.BlockSpec(memory_space=pltpu.VMEM)] * count,
        out_shape=[jax.ShapeDtypeStruct((rows, heads * width), blocks.dtype)] * count,
        cost_estimate=pl.CostEstimate(
            flops=0, transcendentals=0, bytes_accessed=2 * blocks.size * blocks.dtype.itemsize
        ),
    )(blocks)


def per_device(query_rows, key_rows, value_rows, out_grad, out_weight, text_length):
    devices = lax.axis_size("dp")
    tok_rows = query_rows.shape[1]

    def by_heads(array):
        return array[0].reshape(tok_rows, HEADS, HEAD_DIM)

    slot_text = (jnp.arange(devices) * tok_rows < TXT)[:, None, None]
    outgoing = jnp.where(slot_text, out_weight[0][None], out_weight[1][None])
    stream_rows = lax.all_to_all(outgoing, "dp", split_axis=0, concat_axis=0, tiled=True)
    own_half = lax.all_gather(stream_rows, "z", axis=1, tiled=False)
    other_half = lax.ppermute(own_half, "core", [(0, 1), (1, 0)])

    qkv = jnp.stack([by_heads(query_rows), by_heads(key_rows), by_heads(value_rows)])
    qkv_heads = lax.all_to_all(qkv, "dp", split_axis=2, concat_axis=1, tiled=True)

    own_part = jnp.einsum(
        "te,kzre->tkzr", out_grad[0], own_half, preferred_element_type=jnp.float32
    )
    other_part = jnp.einsum(
        "te,kzre->tkzr", out_grad[0], other_half, preferred_element_type=jnp.float32
    )
    first = lax.axis_index("core") == 0
    projected = jnp.stack(
        [jnp.where(first, own_part, other_part), jnp.where(first, other_part, own_part)], axis=3
    ).reshape(tok_rows, HEADS, HEAD_DIM)
    grad_heads = lax.all_to_all(
        projected.astype(jnp.bfloat16), "dp", split_axis=1, concat_axis=0, tiled=True
    )
    total_rows = tok_rows * devices
    query_heads = qkv_heads[0].reshape(total_rows, HEAD_DIM)
    key_heads = qkv_heads[1].reshape(total_rows, HEAD_DIM)
    probs = attention_probs(query_heads, key_heads, text_length)
    query_grad, key_grad, value_grad = attention_grads(
        query_heads,
        key_heads,
        qkv_heads[2].reshape(total_rows, HEAD_DIM),
        grad_heads.reshape(total_rows, HEAD_DIM),
        text_length,
        probs,
    )
    grads = jnp.stack([query_grad, key_grad, value_grad]).reshape(3, devices, tok_rows, HEAD_DIM)
    returned = lax.all_to_all(grads.transpose(1, 0, 2, 3), "dp", split_axis=0, concat_axis=0, tiled=True)
    return tuple(out.reshape(1, tok_rows, HEADS * HEAD_DIM) for out in relayout(returned))


def solution(mesh):
    dp, seq = mesh.shape["dp"], mesh.shape["seq"]
    cores = 2
    split = Mesh(mesh.devices.reshape(dp, seq // cores, cores), ("dp", "z", "core"))
    rows = ("z", "core")
    in_specs = (
        P(rows, "dp", None),
        P(rows, "dp", None),
        P(rows, "dp", None),
        P(rows, "dp", None),
        P(None, ("dp", "z", "core"), None),
        P(rows),
    )
    out_specs = (P(rows, "dp", None), P(rows, "dp", None), P(rows, "dp", None))
    return jax.shard_map(
        per_device, mesh=split, in_specs=in_specs, out_specs=out_specs, check_vma=False
    )
```

```python
import functools
import math

import jax
import jax.numpy as jnp
from jax import lax
from jax.experimental import pallas as pl
from jax.experimental.pallas import tpu as pltpu
from jax.sharding import PartitionSpec as P

HEADS = 16
HEAD_DIM = 128
TXT = 512
BLOCK_ROWS = 256


def softmax_kernel(length_ref, q_ref, k_ref, p_ref):
    factor = 1.0 / math.sqrt(q_ref.shape[1])
    nt = (((1,), (1,)), ((), ()))
    scores = lax.dot_general(q_ref[...], k_ref[...], nt, preferred_element_type=jnp.float32) * factor
    column = lax.broadcasted_iota(jnp.int32, scores.shape, 1)
    valid = (column >= TXT) | (column < length_ref[0])
    scores = jnp.where(valid, scores, -jnp.inf)
    shifted = jnp.exp(scores - jnp.max(scores, axis=1, keepdims=True))
    p_ref[...] = shifted / jnp.sum(shifted, axis=1, keepdims=True)


def attention_probs(query, key, length):
    rows, width = query.shape
    block = min(BLOCK_ROWS, rows)
    return pl.pallas_call(
        softmax_kernel,
        grid=(rows // block,),
        in_specs=[
            pl.BlockSpec(memory_space=pltpu.SMEM),
            pl.BlockSpec((block, width), lambda i: (i, 0)),
            pl.BlockSpec((rows, width), lambda i: (0, 0)),
        ],
        out_specs=pl.BlockSpec((block, rows), lambda i: (i, 0)),
        out_shape=jax.ShapeDtypeStruct((rows, rows), jnp.float32),
        compiler_params=pltpu.CompilerParams(
            dimension_semantics=("arbitrary",), vmem_limit_bytes=48 * 1024 * 1024
        ),
        cost_estimate=pl.CostEstimate(
            flops=2 * rows * rows * width,
            transcendentals=rows * rows,
            bytes_accessed=2 * rows * width * 2 + rows * rows * 4,
        ),
    )(length, query, key)


def gradient_kernel(p_ref, q_ref, k_ref, v_ref, g_ref, dq_ref, dk_ref, dv_ref, dkt_acc, dvt_acc):
    step = pl.program_id(0)
    factor = 1.0 / math.sqrt(q_ref.shape[1])
    nt = (((1,), (1,)), ((), ()))

    @pl.when(step == 0)
    def _():
        dkt_acc[...] = jnp.zeros_like(dkt_acc)
        dvt_acc[...] = jnp.zeros_like(dvt_acc)

    attention = p_ref[...]
    grad_block = g_ref[...]
    keys = k_ref[...]
    attention_low = attention.astype(jnp.bfloat16)
    grad_t = grad_block.astype(jnp.float32).T.astype(jnp.bfloat16)
    dvt_acc[...] += jnp.dot(grad_t, attention_low, preferred_element_type=jnp.float32)
    weight_grad = lax.dot_general(grad_block, v_ref[...], nt, preferred_element_type=jnp.float32)
    row_dot = jnp.sum(attention * weight_grad, axis=1, keepdims=True)
    score_grad = (attention * (weight_grad - row_dot) * factor).astype(jnp.bfloat16)
    dq_ref[...] = jnp.dot(score_grad, keys, preferred_element_type=jnp.float32).astype(dq_ref.dtype)
    query_t = q_ref[...].astype(jnp.float32).T.astype(jnp.bfloat16)
    dkt_acc[...] += jnp.dot(query_t, score_grad, preferred_element_type=jnp.float32)

    @pl.when(step == pl.num_programs(0) - 1)
    def _():
        dk_ref[...] = dkt_acc[...].T.astype(dk_ref.dtype)
        dv_ref[...] = dvt_acc[...].T.astype(dv_ref.dtype)


def attention_grads(query, key, value, grad, length, probs=None):
    rows, width = query.shape
    if probs is None:
        probs = attention_probs(query, key, length)
    block = min(BLOCK_ROWS, rows)
    row_spec = pl.BlockSpec((block, width), lambda i: (i, 0))
    full_spec = pl.BlockSpec((rows, width), lambda i: (0, 0))
    out = jax.ShapeDtypeStruct((rows, width), jnp.bfloat16)
    return pl.pallas_call(
        gradient_kernel,
        grid=(rows // block,),
        in_specs=[
            pl.BlockSpec((block, rows), lambda i: (i, 0)),
            row_spec,
            full_spec,
            full_spec,
            row_spec,
        ],
        out_specs=[row_spec, full_spec, full_spec],
        out_shape=[out, out, out],
        scratch_shapes=[
            pltpu.VMEM((width, rows), jnp.float32),
            pltpu.VMEM((width, rows), jnp.float32),
        ],
        compiler_params=pltpu.CompilerParams(
            dimension_semantics=("arbitrary",), vmem_limit_bytes=48 * 1024 * 1024
        ),
        cost_estimate=pl.CostEstimate(
            flops=8 * rows * rows * width,
            transcendentals=0,
            bytes_accessed=7 * rows * width * 2 + rows * rows * 4,
        ),
    )(probs, query, key, value, grad)


def relayout_kernel(block_ref, *out_refs):
    heads, _, _, width = block_ref.shape
    for index, out_ref in enumerate(out_refs):
        for head in range(heads):
            out_ref[:, head * width : (head + 1) * width] = block_ref[head, index]


def relayout(blocks):
    heads, count, rows, width = blocks.shape
    return pl.pallas_call(
        relayout_kernel,
        in_specs=[pl.BlockSpec(memory_space=pltpu.VMEM)],
        out_specs=[pl.BlockSpec(memory_space=pltpu.VMEM)] * count,
        out_shape=[jax.ShapeDtypeStruct((rows, heads * width), blocks.dtype)] * count,
        cost_estimate=pl.CostEstimate(
            flops=0, transcendentals=0, bytes_accessed=2 * blocks.size * blocks.dtype.itemsize
        ),
    )(blocks)


def per_device(query_rows, key_rows, value_rows, out_grad, out_weight, text_length):
    devices = lax.axis_size("dp")
    tok_rows = query_rows.shape[1]

    def by_heads(array):
        return array[0].reshape(tok_rows, HEADS, HEAD_DIM)

    slot_text = (jnp.arange(devices) * tok_rows < TXT)[:, None, None]
    outgoing = jnp.where(slot_text, out_weight[0][None], out_weight[1][None])
    half = outgoing.shape[1] // 2
    first_rows = lax.all_to_all(outgoing[:, :half], "dp", split_axis=0, concat_axis=0, tiled=True)
    first_weight = lax.all_gather(first_rows, "seq", axis=1, tiled=True)
    second_rows = lax.all_to_all(outgoing[:, half:], "dp", split_axis=0, concat_axis=0, tiled=True)
    second_rows, first_weight = lax.optimization_barrier((second_rows, first_weight))
    second_weight = lax.all_gather(second_rows, "seq", axis=1, tiled=True)

    qkv = jnp.stack([by_heads(query_rows), by_heads(key_rows), by_heads(value_rows)])
    qkv_heads = lax.all_to_all(qkv, "dp", split_axis=2, concat_axis=1, tiled=True)

    parts = [
        jnp.einsum("te,kre->tkr", out_grad[0], weight, preferred_element_type=jnp.float32).reshape(
            tok_rows, HEADS, -1, half
        )
        for weight in (first_weight, second_weight)
    ]
    projected = jnp.concatenate(parts, axis=3).reshape(tok_rows, HEADS, HEAD_DIM)
    grad_heads = lax.all_to_all(
        projected.astype(jnp.bfloat16), "dp", split_axis=1, concat_axis=0, tiled=True
    )
    total_rows = tok_rows * devices
    query_heads = qkv_heads[0].reshape(total_rows, HEAD_DIM)
    key_heads = qkv_heads[1].reshape(total_rows, HEAD_DIM)
    probs = attention_probs(query_heads, key_heads, text_length)
    query_grad, key_grad, value_grad = attention_grads(
        query_heads,
        key_heads,
        qkv_heads[2].reshape(total_rows, HEAD_DIM),
        grad_heads.reshape(total_rows, HEAD_DIM),
        text_length,
        probs,
    )
    grads = jnp.stack([query_grad, key_grad, value_grad]).reshape(3, devices, tok_rows, HEAD_DIM)
    returned = lax.all_to_all(grads.transpose(1, 0, 2, 3), "dp", split_axis=0, concat_axis=0, tiled=True)
    return tuple(out.reshape(1, tok_rows, HEADS * HEAD_DIM) for out in relayout(returned))


def solution(mesh):
    in_specs = (
        P("seq", "dp", None),
        P("seq", "dp", None),
        P("seq", "dp", None),
        P("seq", "dp", None),
        P(None, ("dp", "seq"), None),
        P("seq"),
    )
    out_specs = (P("seq", "dp", None), P("seq", "dp", None), P("seq", "dp", None))
    return jax.shard_map(
        per_device, mesh=mesh, in_specs=in_specs, out_specs=out_specs, check_vma=False
    )
```

```python
import functools
import math

import jax
import jax.numpy as jnp
from jax import lax
from jax.experimental import pallas as pl
from jax.experimental.pallas import tpu as pltpu
from jax.sharding import PartitionSpec as P

HEADS = 16
HEAD_DIM = 128
TXT = 512
BLOCK_ROWS = 256


def softmax_kernel(length_ref, q_ref, k_ref, p_ref):
    factor = 1.0 / math.sqrt(q_ref.shape[1])
    nt = (((1,), (1,)), ((), ()))
    scores = lax.dot_general(q_ref[...], k_ref[...], nt, preferred_element_type=jnp.float32) * factor
    column = lax.broadcasted_iota(jnp.int32, scores.shape, 1)
    valid = (column >= TXT) | (column < length_ref[0])
    scores = jnp.where(valid, scores, -jnp.inf)
    shifted = jnp.exp(scores - jnp.max(scores, axis=1, keepdims=True))
    p_ref[...] = shifted / jnp.sum(shifted, axis=1, keepdims=True)


def attention_probs(query, key, length):
    rows, width = query.shape
    block = min(BLOCK_ROWS, rows)
    return pl.pallas_call(
        softmax_kernel,
        grid=(rows // block,),
        in_specs=[
            pl.BlockSpec(memory_space=pltpu.SMEM),
            pl.BlockSpec((block, width), lambda i: (i, 0)),
            pl.BlockSpec((rows, width), lambda i: (0, 0)),
        ],
        out_specs=pl.BlockSpec((block, rows), lambda i: (i, 0)),
        out_shape=jax.ShapeDtypeStruct((rows, rows), jnp.float32),
        compiler_params=pltpu.CompilerParams(
            dimension_semantics=("arbitrary",), vmem_limit_bytes=48 * 1024 * 1024
        ),
        cost_estimate=pl.CostEstimate(
            flops=2 * rows * rows * width,
            transcendentals=rows * rows,
            bytes_accessed=2 * rows * width * 2 + rows * rows * 4,
        ),
    )(length, query, key)


def gradient_kernel(p_ref, q_ref, k_ref, v_ref, g_ref, dq_ref, dk_ref, dv_ref, dkt_acc, dvt_acc):
    step = pl.program_id(0)
    factor = 1.0 / math.sqrt(q_ref.shape[1])
    nt = (((1,), (1,)), ((), ()))

    @pl.when(step == 0)
    def _():
        dkt_acc[...] = jnp.zeros_like(dkt_acc)
        dvt_acc[...] = jnp.zeros_like(dvt_acc)

    attention = p_ref[...]
    grad_block = g_ref[...]
    keys = k_ref[...]
    attention_low = attention.astype(jnp.bfloat16)
    grad_t = grad_block.astype(jnp.float32).T.astype(jnp.bfloat16)
    dvt_acc[...] += jnp.dot(grad_t, attention_low, preferred_element_type=jnp.float32)
    weight_grad = lax.dot_general(grad_block, v_ref[...], nt, preferred_element_type=jnp.float32)
    row_dot = jnp.sum(attention * weight_grad, axis=1, keepdims=True)
    score_grad = (attention * (weight_grad - row_dot) * factor).astype(jnp.bfloat16)
    dq_ref[...] = jnp.dot(score_grad, keys, preferred_element_type=jnp.float32).astype(dq_ref.dtype)
    query_t = q_ref[...].astype(jnp.float32).T.astype(jnp.bfloat16)
    dkt_acc[...] += jnp.dot(query_t, score_grad, preferred_element_type=jnp.float32)

    @pl.when(step == pl.num_programs(0) - 1)
    def _():
        dk_ref[...] = dkt_acc[...].T.astype(dk_ref.dtype)
        dv_ref[...] = dvt_acc[...].T.astype(dv_ref.dtype)


def attention_grads(query, key, value, grad, length, probs=None):
    rows, width = query.shape
    if probs is None:
        probs = attention_probs(query, key, length)
    block = min(BLOCK_ROWS, rows)
    row_spec = pl.BlockSpec((block, width), lambda i: (i, 0))
    full_spec = pl.BlockSpec((rows, width), lambda i: (0, 0))
    out = jax.ShapeDtypeStruct((rows, width), jnp.bfloat16)
    return pl.pallas_call(
        gradient_kernel,
        grid=(rows // block,),
        in_specs=[
            pl.BlockSpec((block, rows), lambda i: (i, 0)),
            row_spec,
            full_spec,
            full_spec,
            row_spec,
        ],
        out_specs=[row_spec, full_spec, full_spec],
        out_shape=[out, out, out],
        scratch_shapes=[
            pltpu.VMEM((width, rows), jnp.float32),
            pltpu.VMEM((width, rows), jnp.float32),
        ],
        compiler_params=pltpu.CompilerParams(
            dimension_semantics=("arbitrary",), vmem_limit_bytes=48 * 1024 * 1024
        ),
        cost_estimate=pl.CostEstimate(
            flops=8 * rows * rows * width,
            transcendentals=0,
            bytes_accessed=7 * rows * width * 2 + rows * rows * 4,
        ),
    )(probs, query, key, value, grad)


def relayout_kernel(block_ref, *out_refs):
    heads, _, _, width = block_ref.shape
    for index, out_ref in enumerate(out_refs):
        for head in range(heads):
            out_ref[:, head * width : (head + 1) * width] = block_ref[head, index]


def relayout(blocks):
    heads, count, rows, width = blocks.shape
    return pl.pallas_call(
        relayout_kernel,
        in_specs=[pl.BlockSpec(memory_space=pltpu.VMEM)],
        out_specs=[pl.BlockSpec(memory_space=pltpu.VMEM)] * count,
        out_shape=[jax.ShapeDtypeStruct((rows, heads * width), blocks.dtype)] * count,
        cost_estimate=pl.CostEstimate(
            flops=0, transcendentals=0, bytes_accessed=2 * blocks.size * blocks.dtype.itemsize
        ),
    )(blocks)


def per_device(query_rows, key_rows, value_rows, out_grad, out_weight, text_length):
    devices = lax.axis_size("dp")
    tok_rows = query_rows.shape[1]

    def by_heads(array):
        return array[0].reshape(tok_rows, HEADS, HEAD_DIM)

    both_streams = lax.all_gather(out_weight, ("dp", "seq"), axis=1, tiled=True)
    stream = (lax.axis_index("dp") * tok_rows >= TXT).astype(jnp.int32)
    weight = lax.dynamic_index_in_dim(both_streams, stream, 0, keepdims=False).reshape(
        HEADS, -1, out_weight.shape[-1]
    )

    qkv = jnp.stack([by_heads(query_rows), by_heads(key_rows), by_heads(value_rows)])
    qkv_heads = lax.all_to_all(qkv, "dp", split_axis=2, concat_axis=1, tiled=True)

    projected = jnp.einsum(
        "te,kre->tkr", out_grad[0], weight, preferred_element_type=jnp.float32
    )
    grad_heads = lax.all_to_all(
        projected.astype(jnp.bfloat16), "dp", split_axis=1, concat_axis=0, tiled=True
    )
    total_rows = tok_rows * devices
    query_heads = qkv_heads[0].reshape(total_rows, HEAD_DIM)
    key_heads = qkv_heads[1].reshape(total_rows, HEAD_DIM)
    probs = attention_probs(query_heads, key_heads, text_length)
    query_grad, key_grad, value_grad = attention_grads(
        query_heads,
        key_heads,
        qkv_heads[2].reshape(total_rows, HEAD_DIM),
        grad_heads.reshape(total_rows, HEAD_DIM),
        text_length,
        probs,
    )
    grads = jnp.stack([query_grad, key_grad, value_grad]).reshape(3, devices, tok_rows, HEAD_DIM)
    returned = lax.all_to_all(grads.transpose(1, 0, 2, 3), "dp", split_axis=0, concat_axis=0, tiled=True)
    return tuple(out.reshape(1, tok_rows, HEADS * HEAD_DIM) for out in relayout(returned))


def solution(mesh):
    in_specs = (
        P("seq", "dp", None),
        P("seq", "dp", None),
        P("seq", "dp", None),
        P("seq", "dp", None),
        P(None, ("dp", "seq"), None),
        P("seq"),
    )
    out_specs = (P("seq", "dp", None), P("seq", "dp", None), P("seq", "dp", None))
    return jax.shard_map(
        per_device, mesh=mesh, in_specs=in_specs, out_specs=out_specs, check_vma=False
    )
```

```python
import functools
import math

import jax
import jax.numpy as jnp
from jax import lax
from jax.experimental import pallas as pl
from jax.experimental.pallas import tpu as pltpu
from jax.sharding import PartitionSpec as P

HEADS = 16
HEAD_DIM = 128
TXT = 512
BLOCK_ROWS = 512


def softmax_kernel(length_ref, q_ref, k_ref, p_ref):
    factor = 1.0 / math.sqrt(q_ref.shape[1])
    nt = (((1,), (1,)), ((), ()))
    scores = lax.dot_general(q_ref[...], k_ref[...], nt, preferred_element_type=jnp.float32) * factor
    column = lax.broadcasted_iota(jnp.int32, scores.shape, 1)
    valid = (column >= TXT) | (column < length_ref[0])
    scores = jnp.where(valid, scores, -jnp.inf)
    shifted = jnp.exp(scores - jnp.max(scores, axis=1, keepdims=True))
    p_ref[...] = shifted / jnp.sum(shifted, axis=1, keepdims=True)


def attention_probs(query, key, length):
    rows, width = query.shape
    block = min(BLOCK_ROWS, rows)
    return pl.pallas_call(
        softmax_kernel,
        grid=(rows // block,),
        in_specs=[
            pl.BlockSpec(memory_space=pltpu.SMEM),
            pl.BlockSpec((block, width), lambda i: (i, 0)),
            pl.BlockSpec((rows, width), lambda i: (0, 0)),
        ],
        out_specs=pl.BlockSpec((block, rows), lambda i: (i, 0)),
        out_shape=jax.ShapeDtypeStruct((rows, rows), jnp.float32),
        compiler_params=pltpu.CompilerParams(
            dimension_semantics=("arbitrary",), vmem_limit_bytes=48 * 1024 * 1024
        ),
        cost_estimate=pl.CostEstimate(
            flops=2 * rows * rows * width,
            transcendentals=rows * rows,
            bytes_accessed=2 * rows * width * 2 + rows * rows * 4,
        ),
    )(length, query, key)


def gradient_kernel(p_ref, q_ref, k_ref, v_ref, g_ref, dq_ref, dk_ref, dv_ref, dkt_acc, dvt_acc):
    step = pl.program_id(0)
    factor = 1.0 / math.sqrt(q_ref.shape[1])
    nt = (((1,), (1,)), ((), ()))

    @pl.when(step == 0)
    def _():
        dkt_acc[...] = jnp.zeros_like(dkt_acc)
        dvt_acc[...] = jnp.zeros_like(dvt_acc)

    attention = p_ref[...]
    grad_block = g_ref[...]
    keys = k_ref[...]
    attention_low = attention.astype(jnp.bfloat16)
    grad_t = grad_block.astype(jnp.float32).T.astype(jnp.bfloat16)
    dvt_acc[...] += jnp.dot(grad_t, attention_low, preferred_element_type=jnp.float32)
    weight_grad = lax.dot_general(grad_block, v_ref[...], nt, preferred_element_type=jnp.float32)
    row_dot = jnp.sum(attention * weight_grad, axis=1, keepdims=True)
    score_grad = (attention * (weight_grad - row_dot) * factor).astype(jnp.bfloat16)
    dq_ref[...] = jnp.dot(score_grad, keys, preferred_element_type=jnp.float32).astype(dq_ref.dtype)
    query_t = q_ref[...].astype(jnp.float32).T.astype(jnp.bfloat16)
    dkt_acc[...] += jnp.dot(query_t, score_grad, preferred_element_type=jnp.float32)

    @pl.when(step == pl.num_programs(0) - 1)
    def _():
        dk_ref[...] = dkt_acc[...].T.astype(dk_ref.dtype)
        dv_ref[...] = dvt_acc[...].T.astype(dv_ref.dtype)


def attention_grads(query, key, value, grad, length, probs=None):
    rows, width = query.shape
    if probs is None:
        probs = attention_probs(query, key, length)
    block = min(BLOCK_ROWS, rows)
    row_spec = pl.BlockSpec((block, width), lambda i: (i, 0))
    full_spec = pl.BlockSpec((rows, width), lambda i: (0, 0))
    out = jax.ShapeDtypeStruct((rows, width), jnp.bfloat16)
    return pl.pallas_call(
        gradient_kernel,
        grid=(rows // block,),
        in_specs=[
            pl.BlockSpec((block, rows), lambda i: (i, 0)),
            row_spec,
            full_spec,
            full_spec,
            row_spec,
        ],
        out_specs=[row_spec, full_spec, full_spec],
        out_shape=[out, out, out],
        scratch_shapes=[
            pltpu.VMEM((width, rows), jnp.float32),
            pltpu.VMEM((width, rows), jnp.float32),
        ],
        compiler_params=pltpu.CompilerParams(
            dimension_semantics=("arbitrary",), vmem_limit_bytes=48 * 1024 * 1024
        ),
        cost_estimate=pl.CostEstimate(
            flops=8 * rows * rows * width,
            transcendentals=0,
            bytes_accessed=7 * rows * width * 2 + rows * rows * 4,
        ),
    )(probs, query, key, value, grad)


def relayout_kernel(block_ref, *out_refs):
    heads, _, _, width = block_ref.shape
    for index, out_ref in enumerate(out_refs):
        for head in range(heads):
            out_ref[:, head * width : (head + 1) * width] = block_ref[head, index]


def relayout(blocks):
    heads, count, rows, width = blocks.shape
    return pl.pallas_call(
        relayout_kernel,
        in_specs=[pl.BlockSpec(memory_space=pltpu.VMEM)],
        out_specs=[pl.BlockSpec(memory_space=pltpu.VMEM)] * count,
        out_shape=[jax.ShapeDtypeStruct((rows, heads * width), blocks.dtype)] * count,
        cost_estimate=pl.CostEstimate(
            flops=0, transcendentals=0, bytes_accessed=2 * blocks.size * blocks.dtype.itemsize
        ),
    )(blocks)


def per_device(query_rows, key_rows, value_rows, out_grad, out_weight, text_length):
    devices = lax.axis_size("dp")
    tok_rows = query_rows.shape[1]

    def by_heads(array):
        return array[0].reshape(tok_rows, HEADS, HEAD_DIM)

    slot_text = (jnp.arange(devices) * tok_rows < TXT)[:, None, None]
    outgoing = jnp.where(slot_text, out_weight[0][None], out_weight[1][None])
    stream_rows = lax.all_to_all(outgoing, "dp", split_axis=0, concat_axis=0, tiled=True)
    weight = lax.all_gather(stream_rows, "seq", axis=1, tiled=True)

    qkv = jnp.stack([by_heads(query_rows), by_heads(key_rows), by_heads(value_rows)])
    qkv_heads = lax.all_to_all(qkv, "dp", split_axis=2, concat_axis=1, tiled=True)

    projected = jnp.einsum(
        "te,kre->tkr", out_grad[0], weight, preferred_element_type=jnp.float32
    )
    grad_heads = lax.all_to_all(
        projected.astype(jnp.bfloat16), "dp", split_axis=1, concat_axis=0, tiled=True
    )
    total_rows = tok_rows * devices
    query_heads = qkv_heads[0].reshape(total_rows, HEAD_DIM)
    key_heads = qkv_heads[1].reshape(total_rows, HEAD_DIM)
    probs = attention_probs(query_heads, key_heads, text_length)
    query_grad, key_grad, value_grad = attention_grads(
        query_heads,
        key_heads,
        qkv_heads[2].reshape(total_rows, HEAD_DIM),
        grad_heads.reshape(total_rows, HEAD_DIM),
        text_length,
        probs,
    )
    grads = jnp.stack([query_grad, key_grad, value_grad]).reshape(3, devices, tok_rows, HEAD_DIM)
    returned = lax.all_to_all(grads.transpose(1, 0, 2, 3), "dp", split_axis=0, concat_axis=0, tiled=True)
    return tuple(out.reshape(1, tok_rows, HEADS * HEAD_DIM) for out in relayout(returned))


def solution(mesh):
    in_specs = (
        P("seq", "dp", None),
        P("seq", "dp", None),
        P("seq", "dp", None),
        P("seq", "dp", None),
        P(None, ("dp", "seq"), None),
        P("seq"),
    )
    out_specs = (P("seq", "dp", None), P("seq", "dp", None), P("seq", "dp", None))
    return jax.shard_map(
        per_device, mesh=mesh, in_specs=in_specs, out_specs=out_specs, check_vma=False
    )
```

```python
import functools
import math

import jax
import jax.numpy as jnp
from jax import lax
from jax.experimental import pallas as pl
from jax.experimental.pallas import tpu as pltpu
from jax.sharding import PartitionSpec as P

HEADS = 16
HEAD_DIM = 128
TXT = 512
BLOCK_ROWS = 1024


def softmax_kernel(length_ref, q_ref, k_ref, p_ref):
    factor = 1.0 / math.sqrt(q_ref.shape[1])
    nt = (((1,), (1,)), ((), ()))
    scores = lax.dot_general(q_ref[...], k_ref[...], nt, preferred_element_type=jnp.float32) * factor
    column = lax.broadcasted_iota(jnp.int32, scores.shape, 1)
    valid = (column >= TXT) | (column < length_ref[0])
    scores = jnp.where(valid, scores, -jnp.inf)
    shifted = jnp.exp(scores - jnp.max(scores, axis=1, keepdims=True))
    p_ref[...] = shifted / jnp.sum(shifted, axis=1, keepdims=True)


def attention_probs(query, key, length):
    rows, width = query.shape
    block = min(BLOCK_ROWS, rows)
    return pl.pallas_call(
        softmax_kernel,
        grid=(rows // block,),
        in_specs=[
            pl.BlockSpec(memory_space=pltpu.SMEM),
            pl.BlockSpec((block, width), lambda i: (i, 0)),
            pl.BlockSpec((rows, width), lambda i: (0, 0)),
        ],
        out_specs=pl.BlockSpec((block, rows), lambda i: (i, 0)),
        out_shape=jax.ShapeDtypeStruct((rows, rows), jnp.float32),
        compiler_params=pltpu.CompilerParams(
            dimension_semantics=("arbitrary",), vmem_limit_bytes=48 * 1024 * 1024
        ),
        cost_estimate=pl.CostEstimate(
            flops=2 * rows * rows * width,
            transcendentals=rows * rows,
            bytes_accessed=2 * rows * width * 2 + rows * rows * 4,
        ),
    )(length, query, key)


def gradient_kernel(p_ref, q_ref, k_ref, v_ref, g_ref, dq_ref, dk_ref, dv_ref, dkt_acc, dvt_acc):
    step = pl.program_id(0)
    factor = 1.0 / math.sqrt(q_ref.shape[1])
    nt = (((1,), (1,)), ((), ()))

    @pl.when(step == 0)
    def _():
        dkt_acc[...] = jnp.zeros_like(dkt_acc)
        dvt_acc[...] = jnp.zeros_like(dvt_acc)

    attention = p_ref[...]
    grad_block = g_ref[...]
    keys = k_ref[...]
    attention_low = attention.astype(jnp.bfloat16)
    grad_t = grad_block.astype(jnp.float32).T.astype(jnp.bfloat16)
    dvt_acc[...] += jnp.dot(grad_t, attention_low, preferred_element_type=jnp.float32)
    weight_grad = lax.dot_general(grad_block, v_ref[...], nt, preferred_element_type=jnp.float32)
    row_dot = jnp.sum(attention * weight_grad, axis=1, keepdims=True)
    score_grad = (attention * (weight_grad - row_dot) * factor).astype(jnp.bfloat16)
    dq_ref[...] = jnp.dot(score_grad, keys, preferred_element_type=jnp.float32).astype(dq_ref.dtype)
    query_t = q_ref[...].astype(jnp.float32).T.astype(jnp.bfloat16)
    dkt_acc[...] += jnp.dot(query_t, score_grad, preferred_element_type=jnp.float32)

    @pl.when(step == pl.num_programs(0) - 1)
    def _():
        dk_ref[...] = dkt_acc[...].T.astype(dk_ref.dtype)
        dv_ref[...] = dvt_acc[...].T.astype(dv_ref.dtype)


def attention_grads(query, key, value, grad, length, probs=None):
    rows, width = query.shape
    if probs is None:
        probs = attention_probs(query, key, length)
    block = min(BLOCK_ROWS, rows)
    row_spec = pl.BlockSpec((block, width), lambda i: (i, 0))
    full_spec = pl.BlockSpec((rows, width), lambda i: (0, 0))
    out = jax.ShapeDtypeStruct((rows, width), jnp.bfloat16)
    return pl.pallas_call(
        gradient_kernel,
        grid=(rows // block,),
        in_specs=[
            pl.BlockSpec((block, rows), lambda i: (i, 0)),
            row_spec,
            full_spec,
            full_spec,
            row_spec,
        ],
        out_specs=[row_spec, full_spec, full_spec],
        out_shape=[out, out, out],
        scratch_shapes=[
            pltpu.VMEM((width, rows), jnp.float32),
            pltpu.VMEM((width, rows), jnp.float32),
        ],
        compiler_params=pltpu.CompilerParams(
            dimension_semantics=("arbitrary",), vmem_limit_bytes=48 * 1024 * 1024
        ),
        cost_estimate=pl.CostEstimate(
            flops=8 * rows * rows * width,
            transcendentals=0,
            bytes_accessed=7 * rows * width * 2 + rows * rows * 4,
        ),
    )(probs, query, key, value, grad)


def relayout_kernel(block_ref, *out_refs):
    heads, _, _, width = block_ref.shape
    for index, out_ref in enumerate(out_refs):
        for head in range(heads):
            out_ref[:, head * width : (head + 1) * width] = block_ref[head, index]


def relayout(blocks):
    heads, count, rows, width = blocks.shape
    return pl.pallas_call(
        relayout_kernel,
        in_specs=[pl.BlockSpec(memory_space=pltpu.VMEM)],
        out_specs=[pl.BlockSpec(memory_space=pltpu.VMEM)] * count,
        out_shape=[jax.ShapeDtypeStruct((rows, heads * width), blocks.dtype)] * count,
        cost_estimate=pl.CostEstimate(
            flops=0, transcendentals=0, bytes_accessed=2 * blocks.size * blocks.dtype.itemsize
        ),
    )(blocks)


def per_device(query_rows, key_rows, value_rows, out_grad, out_weight, text_length):
    devices = lax.axis_size("dp")
    tok_rows = query_rows.shape[1]

    def by_heads(array):
        return array[0].reshape(tok_rows, HEADS, HEAD_DIM)

    slot_text = (jnp.arange(devices) * tok_rows < TXT)[:, None, None]
    outgoing = jnp.where(slot_text, out_weight[0][None], out_weight[1][None])
    stream_rows = lax.all_to_all(outgoing, "dp", split_axis=0, concat_axis=0, tiled=True)
    weight = lax.all_gather(stream_rows, "seq", axis=1, tiled=True)

    qkv = jnp.stack([by_heads(query_rows), by_heads(key_rows), by_heads(value_rows)])
    qkv_heads = lax.all_to_all(qkv, "dp", split_axis=2, concat_axis=1, tiled=True)

    projected = jnp.einsum(
        "te,kre->tkr", out_grad[0], weight, preferred_element_type=jnp.float32
    )
    grad_heads = lax.all_to_all(
        projected.astype(jnp.bfloat16), "dp", split_axis=1, concat_axis=0, tiled=True
    )
    total_rows = tok_rows * devices
    query_heads = qkv_heads[0].reshape(total_rows, HEAD_DIM)
    key_heads = qkv_heads[1].reshape(total_rows, HEAD_DIM)
    probs = attention_probs(query_heads, key_heads, text_length)
    query_grad, key_grad, value_grad = attention_grads(
        query_heads,
        key_heads,
        qkv_heads[2].reshape(total_rows, HEAD_DIM),
        grad_heads.reshape(total_rows, HEAD_DIM),
        text_length,
        probs,
    )
    grads = jnp.stack([query_grad, key_grad, value_grad]).reshape(3, devices, tok_rows, HEAD_DIM)
    returned = lax.all_to_all(grads.transpose(1, 0, 2, 3), "dp", split_axis=0, concat_axis=0, tiled=True)
    return tuple(out.reshape(1, tok_rows, HEADS * HEAD_DIM) for out in relayout(returned))


def solution(mesh):
    in_specs = (
        P("seq", "dp", None),
        P("seq", "dp", None),
        P("seq", "dp", None),
        P("seq", "dp", None),
        P(None, ("dp", "seq"), None),
        P("seq"),
    )
    out_specs = (P("seq", "dp", None), P("seq", "dp", None), P("seq", "dp", None))
    return jax.shard_map(
        per_device, mesh=mesh, in_specs=in_specs, out_specs=out_specs, check_vma=False
    )
```
